256 devices in a mesh: gx: 32 (over z_hi, y, core), gy: 8 (over z_lo, x).
Axes of the slice: x: 4, y: 4, z: 8 (z_hi: 4, z_lo: 2; z = z_hi * 2 + z_lo), core: 2. Of those that a mesh axis runs over, the one named last changes fastest.
Arguments:
- state: float32 [5, 256, 64, 128], P(None, 'gx', 'gy'), may hold values from -6 to 6
- terrain: int32 [256, 64], P('gx', 'gy'), may hold values from 0 to 31
- site_cells: int32 [65536], P(('gx', 'gy')), may hold values from 0 to 8191
- site_values: float32 [5, 65536], P(None, ('gx', 'gy')), may hold values from -6 to 6
- w_in: float32 [64, 4], replicated, may hold values from -3 to 3
- b_in: float32 [64], replicated, may hold values from -3 to 3
- w_out: float32 [64], replicated, may hold values from -1.5 to 1.5
Outputs:
- state_grad: float32 [5, 256, 64, 128], P(None, 'gx', 'gy')
- closure_grad: float32 [64, 6], replicated
The draws below stay inside these ranges and needn't reach their ends.
Inputs may be any that keep to these rules, and one draw needn't show every extreme that they name: `site_cells`: site s lies on the device that holds entry s; its id names a cell of that device's block as (i * 8 + j) * 128 + k for local position (i, j, k).
All inputs are finite; a program needn't handle non-finite values.
Results may differ from the reference program's by a relative error of at most 0.0003.
Values sent between devices are 32-bit elements; how exact they have to be, the bound alone decides.
No kernel may reach another device: no remote copies, remote signals or barrier semaphores. Data moves between devices by JAX's collectives and lax.ppermute only.
A program may use at most 128 MiB of HBM per device.

```python
import jax
import jax.numpy as jnp
from jax import lax

NF = 5
FEAT = 4
HIDDEN_SIZE = 64
NZ = 128
STEPS = 4
CX = 8
CY = 8
SITE_DEV = 256
NX = 256
NY = 64
SITES = 65536
N_GY = 8


def with_ends(drawn, key, least, high):
    extent = drawn.shape
    place = [jax.random.randint(jax.random.fold_in(key, axis), (), 0, extent[axis]) for axis in range(len(extent))]
    drawn = drawn.at[tuple(place)].set(least)
    longest = extent.index(max(extent))
    place[longest] = (place[longest] + 1) % extent[longest]
    return drawn.at[tuple(place)].set(high)


def level_of(stream_key, extent, cuts, smallest, largest):
    factor_of = 1.0
    for axis_at, blocks in cuts:
        draws = jax.random.uniform(jax.random.fold_in(jax.random.fold_in(stream_key, 6), axis_at), (blocks,), jnp.float32, smallest / len(cuts), largest / len(cuts))
        factor_of = factor_of * jnp.repeat(jnp.exp(draws), extent[axis_at] // blocks).reshape((-1,) + (1,) * (len(extent) - 1 - axis_at))
    return factor_of


def noise(rng, dims, width, reach, pieces=(), held_as=jnp.bfloat16):
    level = level_of(rng, dims, pieces, -0.22, 0.18) if pieces else 1.0
    drawn = jax.random.normal(rng, dims, jnp.float32) * width * level
    return jnp.minimum(jnp.maximum(drawn, -reach), reach).astype(held_as)


def setup_inputs(seed: int = 0) -> dict:
    key_of = jax.random.split(jax.random.key(seed), 8)
    state = noise(key_of[0], (NF, NX, NY, NZ), 1.0, 6.0, ((1, 32), (2, 8)), jnp.float32)
    terrain = with_ends(jax.random.randint(key_of[1], (NX, NY), 0, NZ // 4), jax.random.fold_in(key_of[1], 1), 0, (NZ // 4) - 1).astype(jnp.int32)
    site_cells = with_ends(jax.random.randint(key_of[2], (SITES,), 0, CX * CY * NZ), jax.random.fold_in(key_of[2], 1), 0, (CX * CY * NZ) - 1).astype(jnp.int32)
    site_values = noise(key_of[3], (NF, SITES), 1.0, 6.0, ((1, 256),), jnp.float32)
    w_in = noise(key_of[4], (HIDDEN_SIZE, FEAT), FEAT ** -0.5, 3.0, (), jnp.float32)
    b_in = noise(key_of[5], (HIDDEN_SIZE,), 0.5, 3.0, (), jnp.float32)
    w_out = noise(key_of[6], (HIDDEN_SIZE,), (HIDDEN_SIZE // 4) ** -0.5, 1.5, (), jnp.float32)
    return {"state": state, "terrain": terrain, "site_cells": site_cells, "site_values": site_values, "w_in": w_in, "b_in": b_in, "w_out": w_out}


PRECISE = lax.Precision.HIGHEST

def vertical_diff(values):
    blank = jnp.zeros_like(values[..., :1])
    upper = jnp.concatenate([values[..., 1:], blank], axis=-1)
    lower = jnp.concatenate([blank, values[..., :-1]], axis=-1)
    return 0.5 * (upper - lower)

def closure_inputs(fields, terrain):
    levels = jnp.arange(fields.shape[-1], dtype=jnp.int32)
    height = 2.0 * (levels - terrain[..., None]).astype(jnp.float32) / fields.shape[-1]
    return jnp.stack([vertical_diff(fields[0]), vertical_diff(fields[1]), vertical_diff(fields[2]), height])

def hidden_units(inputs, w_in, b_in):
    before = jnp.einsum('hf,f...->h...', w_in, inputs, precision=PRECISE)
    return jnp.tanh(before + b_in.reshape((-1,) + (1,) * (inputs.ndim - 1)))

def viscosity(hidden, w_out):
    logit = jnp.einsum('h,h...->...', w_out, hidden, precision=PRECISE)
    return 0.16 * jax.nn.sigmoid(logit)

def row_viscosity(pair, w_in, b_in, w_out):
    fields, terrain = pair
    return viscosity(hidden_units(closure_inputs(fields, terrain), w_in, b_in), w_out)

def column_viscosity(state, terrain, w_in, b_in, w_out):
    rows = jnp.moveaxis(state, 1, 0)
    saver = jax.checkpoint(row_viscosity)
    return lax.map(lambda pair: saver(pair, w_in, b_in, w_out), (rows, terrain))

def next_along(values, axis):
    size = values.shape[axis]
    tail = lax.slice_in_dim(values, 1, size, axis=axis)
    shape = list(values.shape)
    shape[axis] = 1
    return jnp.concatenate([tail, jnp.zeros(shape, values.dtype)], axis=axis)

def prev_along(values, axis):
    size = values.shape[axis]
    head = lax.slice_in_dim(values, 0, size - 1, axis=axis)
    shape = list(values.shape)
    shape[axis] = 1
    return jnp.concatenate([jnp.zeros(shape, values.dtype), head], axis=axis)

def advance(state, viscous, fluid):
    summed = state
    for axis in range(3):
        conductance = fluid * next_along(fluid, axis) * 0.5 * (viscous + next_along(viscous, axis))
        face_flux = conductance * (next_along(state, axis + 1) - state)
        summed = summed + face_flux - prev_along(face_flux, axis + 1)
    return summed

def reference(state, terrain, site_cells, site_values, w_in, b_in, w_out):
    levels = jnp.arange(NZ, dtype=jnp.int32)
    fluid = (levels[None, None, :] >= terrain[:, :, None]).astype(jnp.float32)

    def forward(start, w_first, b_first, w_last):
        fields = start
        for step_index in range(STEPS):
            viscous = jax.checkpoint(column_viscosity)(fields, terrain, w_first, b_first, w_last)
            fields = advance(fields, viscous, fluid)
        return fields
    final, pullback = jax.vjp(forward, state, w_in, b_in, w_out)
    order = jnp.arange(SITES, dtype=jnp.int32)
    device = order // SITE_DEV
    block_x = device // N_GY
    block_y = device % N_GY
    local_x = site_cells // (CY * NZ)
    local_y = site_cells // NZ % CY
    level = site_cells % NZ
    global_ids = (((block_x * CX + local_x) * NY + block_y * CY + local_y) * NZ + level).astype(jnp.int32)
    flat = final.reshape(NF, -1)
    misfit = flat[:, global_ids] - site_values
    adjoint_start = jnp.zeros_like(flat).at[:, global_ids].add(misfit).reshape(final.shape)
    grad_state, grad_in, grad_bias, grad_out = pullback(adjoint_start)
    closure_grad = jnp.concatenate([grad_in, grad_bias[:, None], grad_out[:, None]], axis=1) * SITES ** (-0.5)
    return (grad_state, closure_grad)
```

```python
import jax
import jax.numpy as jnp
from jax import lax
from jax.sharding import PartitionSpec as P

STEPS = 4


PRECISE = lax.Precision.HIGHEST


def padded_2(cells, sides, width):
    for axis, dim in sides:
        count = lax.axis_size(axis)
        ends = count - 1
        head = lax.slice_in_dim(cells, 0, width, axis=dim)
        tail = lax.slice_in_dim(cells, cells.shape[dim] - width, cells.shape[dim], axis=dim)
        cells = jnp.concatenate(
            [
                lax.ppermute(tail, axis, [(i, (i + 1) % count) for i in range(ends)]),
                cells,
                lax.ppermute(head, axis, [((i + 1) % count, i) for i in range(ends)]),
            ],
            axis=dim,
        )
    return cells


def vertical_diff(values):
    blank = jnp.zeros_like(values[..., :1])
    upper = jnp.concatenate([values[..., 1:], blank], axis=-1)
    lower = jnp.concatenate([blank, values[..., :-1]], axis=-1)
    return 0.5 * (upper - lower)


def closure_inputs(fields, terrain):
    levels = jnp.arange(fields.shape[-1], dtype=jnp.int32)
    height = 2.0 * (levels - terrain[..., None]).astype(jnp.float32) / fields.shape[-1]
    return jnp.stack(
        [vertical_diff(fields[0]), vertical_diff(fields[1]), vertical_diff(fields[2]), height]
    )


def hidden_units(inputs, w_in, b_in):
    before = jnp.einsum("hf,f...->h...", w_in, inputs, precision=PRECISE)
    return jnp.tanh(before + b_in.reshape((-1,) + (1,) * (inputs.ndim - 1)))


def viscosity(hidden, w_out):
    logit = jnp.einsum("h,h...->...", w_out, hidden, precision=PRECISE)
    return 0.16 * jax.nn.sigmoid(logit)


def interior(values):
    return values[..., 1:-1, 1:-1, :]


def beside(values):
    return [
        values[..., 2:, 1:-1, :],
        values[..., :-2, 1:-1, :],
        values[..., 1:-1, 2:, :],
        values[..., 1:-1, :-2, :],
    ]


def above_below(values):
    blank = jnp.zeros_like(values[..., :1])
    return [
        jnp.concatenate([values[..., 1:], blank], axis=-1),
        jnp.concatenate([blank, values[..., :-1]], axis=-1),
    ]


def fluid_cells(terrain, levels_count):
    levels = jnp.arange(levels_count, dtype=jnp.int32)
    return (levels >= terrain[..., None]).astype(jnp.float32)


def advance(fields, viscous, fluid):
    centre = interior(fields)
    visc_mid = interior(viscous)
    fluid_mid = interior(fluid)
    near_sets = list(zip(beside(fields), beside(viscous), beside(fluid)))
    near_sets = near_sets + list(
        zip(above_below(centre), above_below(visc_mid), above_below(fluid_mid))
    )
    summed = centre
    for field_near, visc_near, fluid_near in near_sets:
        conductance = fluid_mid * fluid_near * 0.5 * (visc_mid + visc_near)
        summed = summed + conductance * (field_near - centre)
    return summed


def adjoint_step(padded, viscous, fluid, terrain, backward, w_in, b_in, w_out):
    centre = interior(padded)
    visc_mid = interior(viscous)
    fluid_mid = interior(fluid)
    back_mid = interior(backward)
    near_sets = list(zip(beside(padded), beside(viscous), beside(fluid), beside(backward)))
    near_sets = near_sets + list(
        zip(
            above_below(centre),
            above_below(visc_mid),
            above_below(fluid_mid),
            above_below(back_mid),
        )
    )
    result = back_mid
    visc_grad = jnp.zeros(visc_mid.shape, jnp.float32)
    for field_near, visc_near, fluid_near, back_near in near_sets:
        open_face = fluid_mid * fluid_near
        conductance = open_face * 0.5 * (visc_mid + visc_near)
        result = result + conductance * (back_near - back_mid)
        visc_grad = visc_grad + open_face * 0.5 * jnp.sum(
            (field_near - centre) * (back_mid - back_near), axis=0
        )
    inputs = closure_inputs(centre, terrain[1:-1, 1:-1])
    hidden = hidden_units(inputs, w_in, b_in)
    logit = jnp.einsum("h,h...->...", w_out, hidden, precision=PRECISE)
    squash = jax.nn.sigmoid(logit)
    logit_grad = visc_grad * 0.16 * squash * (1.0 - squash)
    before_grad = w_out[:, None, None, None] * logit_grad * (1.0 - hidden * hidden)
    out_grad = jnp.einsum("...,h...->h", logit_grad, hidden, precision=PRECISE)
    in_grad = jnp.einsum("h...,f...->hf", before_grad, inputs, precision=PRECISE)
    bias_grad = jnp.sum(before_grad, axis=(1, 2, 3))
    input_grad = jnp.einsum("hf,h...->f...", w_in, before_grad, precision=PRECISE)
    result = result.at[:3].add(-vertical_diff(input_grad[:3]))
    partial_grad = jnp.concatenate([in_grad, bias_grad[:, None], out_grad[:, None]], axis=1)
    return (result, partial_grad)


def seed_from(final, site_cells, site_values):
    flat = final.reshape(final.shape[0], -1)
    misfit = flat[:, site_cells] - site_values
    return jnp.zeros_like(flat).at[:, site_cells].add(misfit).reshape(final.shape)


def add_partial(grad_sum, partial_grad):
    return grad_sum + partial_grad


def butterfly_sum(values, axis):
    count = lax.axis_size(axis)
    if count & (count - 1):
        return lax.psum(values, axis)
    step = 1
    while step < count:
        values = values + lax.ppermute(values, axis, [(i, i ^ step) for i in range(count)])
        step *= 2
    return values


def body(state, terrain, site_cells, site_values, w_in, b_in, w_out):
    fields_count, width_x, width_y, levels_count = state.shape
    top_code = levels_count - terrain
    grad_sum = jnp.zeros((w_in.shape[0], w_in.shape[1] + 2), jnp.float32)
    saved = []
    code_padded = padded_2(top_code, (("gx", 0), ("gy", 1)), 1)
    terrain_padded = levels_count - code_padded
    fluid_padded = fluid_cells(terrain_padded, levels_count)
    fields = state
    for step_index in range(STEPS):
        padded = padded_2(fields, (("gx", 1), ("gy", 2)), 1)
        viscous = viscosity(hidden_units(closure_inputs(padded, terrain_padded), w_in, b_in), w_out)
        saved.append((padded, viscous, fluid_padded, terrain_padded))
        fields = advance(padded, viscous, fluid_padded)
    backward = seed_from(fields, site_cells, site_values)
    for step_index in range(STEPS - 1, -1, -1):
        padded, viscous, fluid_padded, terrain_padded = saved[step_index]
        back_padded = padded_2(backward, (("gx", 1), ("gy", 2)), 1)
        backward, partial_grad = adjoint_step(
            padded, viscous, fluid_padded, terrain_padded, back_padded, w_in, b_in, w_out
        )
        grad_sum = add_partial(grad_sum, partial_grad)
    closure_sum = butterfly_sum(butterfly_sum(grad_sum, "gy"), "gx")
    site_total = site_cells.shape[0] * lax.axis_size("gx") * lax.axis_size("gy")
    return (backward, closure_sum * site_total ** (-0.5))


def solution(mesh):
    return jax.shard_map(
        body,
        mesh=mesh,
        in_specs=(
            P(None, "gx", "gy", None),
            P("gx", "gy"),
            P(("gx", "gy")),
            P(None, ("gx", "gy")),
            P(),
            P(),
            P(),
        ),
        out_specs=(P(None, "gx", "gy", None), P()),
        check_vma=False,
    )
```

```python
import jax
import jax.numpy as jnp
from jax import lax
from jax.sharding import PartitionSpec as P

STEPS = 4


PRECISE = lax.Precision.HIGHEST


def padded_2(cells, sides, width):
    for axis, dim in sides:
        count = lax.axis_size(axis)
        ends = count - 1
        head = lax.slice_in_dim(cells, 0, width, axis=dim)
        tail = lax.slice_in_dim(cells, cells.shape[dim] - width, cells.shape[dim], axis=dim)
        cells = jnp.concatenate(
            [
                lax.ppermute(tail, axis, [(i, (i + 1) % count) for i in range(ends)]),
                cells,
                lax.ppermute(head, axis, [((i + 1) % count, i) for i in range(ends)]),
            ],
            axis=dim,
        )
    return cells


def vertical_diff(values):
    blank = jnp.zeros_like(values[..., :1])
    upper = jnp.concatenate([values[..., 1:], blank], axis=-1)
    lower = jnp.concatenate([blank, values[..., :-1]], axis=-1)
    return 0.5 * (upper - lower)


def closure_inputs(fields, terrain):
    levels = jnp.arange(fields.shape[-1], dtype=jnp.int32)
    height = 2.0 * (levels - terrain[..., None]).astype(jnp.float32) / fields.shape[-1]
    return jnp.stack(
        [vertical_diff(fields[0]), vertical_diff(fields[1]), vertical_diff(fields[2]), height]
    )


def hidden_units(inputs, w_in, b_in):
    before = jnp.einsum("hf,f...->h...", w_in, inputs, precision=PRECISE)
    return jnp.tanh(before + b_in.reshape((-1,) + (1,) * (inputs.ndim - 1)))


def viscosity(hidden, w_out):
    logit = jnp.einsum("h,h...->...", w_out, hidden, precision=PRECISE)
    return 0.16 * jax.nn.sigmoid(logit)


def interior(values):
    return values[..., 1:-1, 1:-1, :]


def beside(values):
    return [
        values[..., 2:, 1:-1, :],
        values[..., :-2, 1:-1, :],
        values[..., 1:-1, 2:, :],
        values[..., 1:-1, :-2, :],
    ]


def above_below(values):
    blank = jnp.zeros_like(values[..., :1])
    return [
        jnp.concatenate([values[..., 1:], blank], axis=-1),
        jnp.concatenate([blank, values[..., :-1]], axis=-1),
    ]


def fluid_cells(terrain, levels_count):
    levels = jnp.arange(levels_count, dtype=jnp.int32)
    return (levels >= terrain[..., None]).astype(jnp.float32)


def advance(fields, viscous, fluid):
    centre = interior(fields)
    visc_mid = interior(viscous)
    fluid_mid = interior(fluid)
    near_sets = list(zip(beside(fields), beside(viscous), beside(fluid)))
    near_sets = near_sets + list(
        zip(above_below(centre), above_below(visc_mid), above_below(fluid_mid))
    )
    summed = centre
    for field_near, visc_near, fluid_near in near_sets:
        conductance = fluid_mid * fluid_near * 0.5 * (visc_mid + visc_near)
        summed = summed + conductance * (field_near - centre)
    return summed


def crop(values, count, first):
    if count == 0:
        return values
    for dim in (first, first + 1):
        values = lax.slice_in_dim(values, count, values.shape[dim] - count, axis=dim)
    return values


def adjoint_step(padded, viscous, fluid, terrain, backward, w_in, b_in, w_out, core):
    centre = interior(padded)
    visc_mid = interior(viscous)
    fluid_mid = interior(fluid)
    back_mid = interior(backward)
    near_sets = list(zip(beside(padded), beside(viscous), beside(fluid), beside(backward)))
    near_sets = near_sets + list(
        zip(
            above_below(centre),
            above_below(visc_mid),
            above_below(fluid_mid),
            above_below(back_mid),
        )
    )
    result = back_mid
    visc_grad = jnp.zeros(visc_mid.shape, jnp.float32)
    for field_near, visc_near, fluid_near, back_near in near_sets:
        open_face = fluid_mid * fluid_near
        conductance = open_face * 0.5 * (visc_mid + visc_near)
        result = result + conductance * (back_near - back_mid)
        visc_grad = visc_grad + open_face * 0.5 * jnp.sum(
            (field_near - centre) * (back_mid - back_near), axis=0
        )
    inputs = closure_inputs(centre, terrain[1:-1, 1:-1])
    hidden = hidden_units(inputs, w_in, b_in)
    logit = jnp.einsum("h,h...->...", w_out, hidden, precision=PRECISE)
    squash = jax.nn.sigmoid(logit)
    logit_grad = visc_grad * 0.16 * squash * (1.0 - squash)
    before_grad = w_out[:, None, None, None] * logit_grad * (1.0 - hidden * hidden)
    logit_core = crop(logit_grad, core, 0)
    hidden_core = crop(hidden, core, 1)
    before_core = crop(before_grad, core, 1)
    out_grad = jnp.einsum("...,h...->h", logit_core, hidden_core, precision=PRECISE)
    in_grad = jnp.einsum("h...,f...->hf", before_core, crop(inputs, core, 1), precision=PRECISE)
    bias_grad = jnp.sum(before_core, axis=(1, 2, 3))
    input_grad = jnp.einsum("hf,h...->f...", w_in, before_grad, precision=PRECISE)
    result = result.at[:3].add(-vertical_diff(input_grad[:3]))
    partial_grad = jnp.concatenate([in_grad, bias_grad[:, None], out_grad[:, None]], axis=1)
    return (result, partial_grad)


def seed_from(final, site_cells, site_values):
    flat = final.reshape(final.shape[0], -1)
    misfit = flat[:, site_cells] - site_values
    return jnp.zeros_like(flat).at[:, site_cells].add(misfit).reshape(final.shape)


def add_partial(grad_sum, partial_grad):
    return grad_sum + partial_grad


def butterfly_sum(values, axis):
    count = lax.axis_size(axis)
    if count & (count - 1):
        return lax.psum(values, axis)
    step = 1
    while step < count:
        values = values + lax.ppermute(values, axis, [(i, i ^ step) for i in range(count)])
        step *= 2
    return values


HALO = STEPS + 1
BACK_HALO = 2


def body(state, terrain, site_cells, site_values, w_in, b_in, w_out):
    fields_count, width_x, width_y, levels_count = state.shape
    top_code = (levels_count - terrain).astype(jnp.float32)
    code_plane = jnp.broadcast_to(top_code[None, :, :, None], (1, width_x, width_y, levels_count))
    packed = padded_2(jnp.concatenate([state, code_plane], axis=0), (("gx", 1), ("gy", 2)), HALO)
    fields = packed[:fields_count]
    terrain_padded = levels_count - packed[fields_count, :, :, 0].astype(jnp.int32)
    fluid_padded = fluid_cells(terrain_padded, levels_count)
    grad_sum = jnp.zeros((w_in.shape[0], w_in.shape[1] + 2), jnp.float32)
    saved = []
    for step_index in range(STEPS):
        trim = step_index
        terrain_here = crop(terrain_padded, trim, 0)
        fluid_here = crop(fluid_padded, trim, 0)
        viscous = viscosity(hidden_units(closure_inputs(fields, terrain_here), w_in, b_in), w_out)
        saved.append((fields, viscous, fluid_here, terrain_here))
        fields = advance(fields, viscous, fluid_here)
    fields = crop(fields, HALO - STEPS, 1)
    backward = seed_from(fields, site_cells, site_values)
    reach = 0
    for step_index in range(STEPS - 1, -1, -1):
        if reach == 0:
            reach = min(BACK_HALO, step_index + 1)
            backward = padded_2(backward, (("gx", 1), ("gy", 2)), reach)
        padded, viscous, fluid_here, terrain_here = saved[step_index]
        trim = HALO - step_index - reach
        backward, partial_grad = adjoint_step(
            crop(padded, trim, 1),
            crop(viscous, trim, 0),
            crop(fluid_here, trim, 0),
            crop(terrain_here, trim, 0),
            backward,
            w_in,
            b_in,
            w_out,
            reach - 1,
        )
        reach -= 1
        grad_sum = add_partial(grad_sum, partial_grad)
    closure_sum = butterfly_sum(butterfly_sum(grad_sum, "gy"), "gx")
    site_total = site_cells.shape[0] * lax.axis_size("gx") * lax.axis_size("gy")
    return (backward, closure_sum * site_total ** (-0.5))


def solution(mesh):
    return jax.shard_map(
        body,
        mesh=mesh,
        in_specs=(
            P(None, "gx", "gy", None),
            P("gx", "gy"),
            P(("gx", "gy")),
            P(None, ("gx", "gy")),
            P(),
            P(),
            P(),
        ),
        out_specs=(P(None, "gx", "gy", None), P()),
        check_vma=False,
    )
```

```python
import jax
import jax.numpy as jnp
from jax import lax
from jax.sharding import PartitionSpec as P

STEPS = 4


PRECISE = lax.Precision.HIGHEST


def padded_2(cells, sides, width):
    for axis, dim in sides:
        count = lax.axis_size(axis)
        ends = count - 1
        head = lax.slice_in_dim(cells, 0, width, axis=dim)
        tail = lax.slice_in_dim(cells, cells.shape[dim] - width, cells.shape[dim], axis=dim)
        cells = jnp.concatenate(
            [
                lax.ppermute(tail, axis, [(i, (i + 1) % count) for i in range(ends)]),
                cells,
                lax.ppermute(head, axis, [((i + 1) % count, i) for i in range(ends)]),
            ],
            axis=dim,
        )
    return cells


def vertical_diff(values):
    blank = jnp.zeros_like(values[..., :1])
    upper = jnp.concatenate([values[..., 1:], blank], axis=-1)
    lower = jnp.concatenate([blank, values[..., :-1]], axis=-1)
    return 0.5 * (upper - lower)


def closure_inputs(fields, terrain):
    levels = jnp.arange(fields.shape[-1], dtype=jnp.int32)
    height = 2.0 * (levels - terrain[..., None]).astype(jnp.float32) / fields.shape[-1]
    return jnp.stack(
        [vertical_diff(fields[0]), vertical_diff(fields[1]), vertical_diff(fields[2]), height]
    )


def spread(weights, ndim):
    return weights.reshape(weights.shape + (1,) * ndim)


def hidden_units(inputs, w_in, b_in):
    ndim = inputs.ndim - 1
    before = spread(w_in[:, 0], ndim) * inputs[0]
    for feature in range(1, inputs.shape[0]):
        before = before + spread(w_in[:, feature], ndim) * inputs[feature]
    return jnp.tanh(before + spread(b_in, ndim))


def logit_of(hidden, w_out):
    return jnp.sum(spread(w_out, hidden.ndim - 1) * hidden, axis=0)


def viscosity(hidden, w_out):
    return 0.16 * jax.nn.sigmoid(logit_of(hidden, w_out))


def interior(values):
    return values[..., 1:-1, 1:-1, :]


def beside(values):
    return [
        values[..., 2:, 1:-1, :],
        values[..., :-2, 1:-1, :],
        values[..., 1:-1, 2:, :],
        values[..., 1:-1, :-2, :],
    ]


def above_below(values):
    blank = jnp.zeros_like(values[..., :1])
    return [
        jnp.concatenate([values[..., 1:], blank], axis=-1),
        jnp.concatenate([blank, values[..., :-1]], axis=-1),
    ]


def fluid_cells(terrain, levels_count):
    levels = jnp.arange(levels_count, dtype=jnp.int32)
    return (levels >= terrain[..., None]).astype(jnp.float32)


def advance(fields, viscous, fluid):
    centre = interior(fields)
    visc_mid = interior(viscous)
    fluid_mid = interior(fluid)
    near_sets = list(zip(beside(fields), beside(viscous), beside(fluid)))
    near_sets = near_sets + list(
        zip(above_below(centre), above_below(visc_mid), above_below(fluid_mid))
    )
    summed = centre
    for field_near, visc_near, fluid_near in near_sets:
        conductance = fluid_mid * fluid_near * 0.5 * (visc_mid + visc_near)
        summed = summed + conductance * (field_near - centre)
    return summed


def crop(values, count, first):
    if count == 0:
        return values
    for dim in (first, first + 1):
        values = lax.slice_in_dim(values, count, values.shape[dim] - count, axis=dim)
    return values


def adjoint_step(padded, viscous, fluid, terrain, backward, w_in, b_in, w_out, core):
    centre = interior(padded)
    visc_mid = interior(viscous)
    fluid_mid = interior(fluid)
    back_mid = interior(backward)
    near_sets = list(zip(beside(padded), beside(viscous), beside(fluid), beside(backward)))
    near_sets = near_sets + list(
        zip(
            above_below(centre),
            above_below(visc_mid),
            above_below(fluid_mid),
            above_below(back_mid),
        )
    )
    result = back_mid
    visc_grad = jnp.zeros(visc_mid.shape, jnp.float32)
    for field_near, visc_near, fluid_near, back_near in near_sets:
        open_face = fluid_mid * fluid_near
        conductance = open_face * 0.5 * (visc_mid + visc_near)
        result = result + conductance * (back_near - back_mid)
        visc_grad = visc_grad + open_face * 0.5 * jnp.sum(
            (field_near - centre) * (back_mid - back_near), axis=0
        )
    inputs = closure_inputs(centre, terrain[1:-1, 1:-1])
    hidden = hidden_units(inputs, w_in, b_in)
    squash = jax.nn.sigmoid(logit_of(hidden, w_out))
    logit_grad = visc_grad * 0.16 * squash * (1.0 - squash)
    before_grad = spread(w_out, 3) * logit_grad * (1.0 - hidden * hidden)
    logit_core = crop(logit_grad, core, 0)
    hidden_core = crop(hidden, core, 1)
    before_core = crop(before_grad, core, 1)
    inputs_core = crop(inputs, core, 1)
    cells = (1, 2, 3)
    out_grad = jnp.sum(logit_core * hidden_core, axis=cells)
    in_grad = jnp.stack(
        [jnp.sum(before_core * inputs_core[feature], axis=cells) for feature in range(inputs.shape[0])],
        axis=1,
    )
    bias_grad = jnp.sum(before_core, axis=cells)
    input_grad = jnp.stack(
        [jnp.sum(spread(w_in[:, feature], 3) * before_grad, axis=0) for feature in range(3)]
    )
    result = result.at[:3].add(-vertical_diff(input_grad))
    partial_grad = jnp.concatenate([in_grad, bias_grad[:, None], out_grad[:, None]], axis=1)
    return (result, partial_grad)


def seed_from(final, site_cells, site_values):
    flat = final.reshape(final.shape[0], -1)
    misfit = flat[:, site_cells] - site_values
    return jnp.zeros_like(flat).at[:, site_cells].add(misfit).reshape(final.shape)


def add_partial(grad_sum, partial_grad):
    return grad_sum + partial_grad


def butterfly_sum(values, axis):
    count = lax.axis_size(axis)
    if count & (count - 1):
        return lax.psum(values, axis)
    step = 1
    while step < count:
        values = values + lax.ppermute(values, axis, [(i, i ^ step) for i in range(count)])
        step *= 2
    return values


HALO = STEPS + 1
BACK_HALO = 2


def body(state, terrain, site_cells, site_values, w_in, b_in, w_out):
    fields_count, width_x, width_y, levels_count = state.shape
    top_code = (levels_count - terrain).astype(jnp.float32)
    code_plane = jnp.broadcast_to(top_code[None, :, :, None], (1, width_x, width_y, levels_count))
    packed = padded_2(jnp.concatenate([state, code_plane], axis=0), (("gx", 1), ("gy", 2)), HALO)
    fields = packed[:fields_count]
    terrain_padded = levels_count - packed[fields_count, :, :, 0].astype(jnp.int32)
    fluid_padded = fluid_cells(terrain_padded, levels_count)
    grad_sum = jnp.zeros((w_in.shape[0], w_in.shape[1] + 2), jnp.float32)
    saved = []
    for step_index in range(STEPS):
        trim = step_index
        terrain_here = crop(terrain_padded, trim, 0)
        fluid_here = crop(fluid_padded, trim, 0)
        viscous = viscosity(hidden_units(closure_inputs(fields, terrain_here), w_in, b_in), w_out)
        saved.append((fields, viscous, fluid_here, terrain_here))
        fields = advance(fields, viscous, fluid_here)
    fields = crop(fields, HALO - STEPS, 1)
    backward = seed_from(fields, site_cells, site_values)
    reach = 0
    for step_index in range(STEPS - 1, -1, -1):
        if reach == 0:
            reach = min(BACK_HALO, step_index + 1)
            backward = padded_2(backward, (("gx", 1), ("gy", 2)), reach)
        padded, viscous, fluid_here, terrain_here = saved[step_index]
        trim = HALO - step_index - reach
        backward, partial_grad = adjoint_step(
            crop(padded, trim, 1),
            crop(viscous, trim, 0),
            crop(fluid_here, trim, 0),
            crop(terrain_here, trim, 0),
            backward,
            w_in,
            b_in,
            w_out,
            reach - 1,
        )
        reach -= 1
        grad_sum = add_partial(grad_sum, partial_grad)
    closure_sum = butterfly_sum(butterfly_sum(grad_sum, "gy"), "gx")
    site_total = site_cells.shape[0] * lax.axis_size("gx") * lax.axis_size("gy")
    return (backward, closure_sum * site_total ** (-0.5))


def solution(mesh):
    return jax.shard_map(
        body,
        mesh=mesh,
        in_specs=(
            P(None, "gx", "gy", None),
            P("gx", "gy"),
            P(("gx", "gy")),
            P(None, ("gx", "gy")),
            P(),
            P(),
            P(),
        ),
        out_specs=(P(None, "gx", "gy", None), P()),
        check_vma=False,
    )
```

```python
import jax
import jax.numpy as jnp
from jax import lax
from jax.sharding import PartitionSpec as P

STEPS = 4


PRECISE = lax.Precision.HIGHEST


def padded_2(cells, sides, width):
    for axis, dim in sides:
        count = lax.axis_size(axis)
        ends = count - 1
        head = lax.slice_in_dim(cells, 0, width, axis=dim)
        tail = lax.slice_in_dim(cells, cells.shape[dim] - width, cells.shape[dim], axis=dim)
        cells = jnp.concatenate(
            [
                lax.ppermute(tail, axis, [(i, (i + 1) % count) for i in range(ends)]),
                cells,
                lax.ppermute(head, axis, [((i + 1) % count, i) for i in range(ends)]),
            ],
            axis=dim,
        )
    return cells


def vertical_diff(values):
    blank = jnp.zeros_like(values[..., :1])
    upper = jnp.concatenate([values[..., 1:], blank], axis=-1)
    lower = jnp.concatenate([blank, values[..., :-1]], axis=-1)
    return 0.5 * (upper - lower)


def closure_inputs(fields, terrain):
    levels = jnp.arange(fields.shape[-1], dtype=jnp.int32)
    height = 2.0 * (levels - terrain[..., None]).astype(jnp.float32) / fields.shape[-1]
    return jnp.stack(
        [vertical_diff(fields[0]), vertical_diff(fields[1]), vertical_diff(fields[2]), height]
    )


def spread(weights, ndim):
    return weights.reshape(weights.shape + (1,) * ndim)


def hidden_units(inputs, w_in, b_in):
    ndim = inputs.ndim - 1
    before = spread(w_in[:, 0], ndim) * inputs[0]
    for feature in range(1, inputs.shape[0]):
        before = before + spread(w_in[:, feature], ndim) * inputs[feature]
    return jnp.tanh(before + spread(b_in, ndim))


def logit_of(hidden, w_out):
    return jnp.sum(spread(w_out, hidden.ndim - 1) * hidden, axis=0)


def viscosity(hidden, w_out):
    return 0.16 * jax.nn.sigmoid(logit_of(hidden, w_out))


def interior(values):
    return values[..., 1:-1, 1:-1, :]


def beside(values):
    return [
        values[..., 2:, 1:-1, :],
        values[..., :-2, 1:-1, :],
        values[..., 1:-1, 2:, :],
        values[..., 1:-1, :-2, :],
    ]


def above_below(values):
    blank = jnp.zeros_like(values[..., :1])
    return [
        jnp.concatenate([values[..., 1:], blank], axis=-1),
        jnp.concatenate([blank, values[..., :-1]], axis=-1),
    ]


def fluid_cells(terrain, levels_count):
    levels = jnp.arange(levels_count, dtype=jnp.int32)
    return (levels >= terrain[..., None]).astype(jnp.float32)


def advance(fields, viscous, fluid):
    centre = interior(fields)
    visc_mid = interior(viscous)
    fluid_mid = interior(fluid)
    near_sets = list(zip(beside(fields), beside(viscous), beside(fluid)))
    near_sets = near_sets + list(
        zip(above_below(centre), above_below(visc_mid), above_below(fluid_mid))
    )
    summed = centre
    for field_near, visc_near, fluid_near in near_sets:
        conductance = fluid_mid * fluid_near * 0.5 * (visc_mid + visc_near)
        summed = summed + conductance * (field_near - centre)
    return summed


def crop(values, count, first):
    if count == 0:
        return values
    for dim in (first, first + 1):
        values = lax.slice_in_dim(values, count, values.shape[dim] - count, axis=dim)
    return values


def adjoint_step(padded, viscous, fluid, terrain, backward, w_in, b_in, w_out, core):
    centre = interior(padded)
    visc_mid = interior(viscous)
    fluid_mid = interior(fluid)
    back_mid = interior(backward)
    near_sets = list(zip(beside(padded), beside(viscous), beside(fluid), beside(backward)))
    near_sets = near_sets + list(
        zip(
            above_below(centre),
            above_below(visc_mid),
            above_below(fluid_mid),
            above_below(back_mid),
        )
    )
    result = back_mid
    visc_grad = jnp.zeros(visc_mid.shape, jnp.float32)
    for field_near, visc_near, fluid_near, back_near in near_sets:
        open_face = fluid_mid * fluid_near
        conductance = open_face * 0.5 * (visc_mid + visc_near)
        result = result + conductance * (back_near - back_mid)
        visc_grad = visc_grad + open_face * 0.5 * jnp.sum(
            (field_near - centre) * (back_mid - back_near), axis=0
        )
    inputs = closure_inputs(centre, terrain[1:-1, 1:-1])
    hidden = hidden_units(inputs, w_in, b_in)
    squash = jax.nn.sigmoid(logit_of(hidden, w_out))
    logit_grad = visc_grad * 0.16 * squash * (1.0 - squash)
    before_grad = spread(w_out, 3) * logit_grad * (1.0 - hidden * hidden)
    logit_core = crop(logit_grad, core, 0)
    hidden_core = crop(hidden, core, 1)
    before_core = crop(before_grad, core, 1)
    inputs_core = crop(inputs, core, 1)
    cells = (1, 2, 3)
    out_grad = jnp.sum(logit_core * hidden_core, axis=cells)
    in_grad = jnp.stack(
        [jnp.sum(before_core * inputs_core[feature], axis=cells) for feature in range(inputs.shape[0])],
        axis=1,
    )
    bias_grad = jnp.sum(before_core, axis=cells)
    input_grad = jnp.stack(
        [jnp.sum(spread(w_in[:, feature], 3) * before_grad, axis=0) for feature in range(3)]
    )
    result = result.at[:3].add(-vertical_diff(input_grad))
    partial_grad = jnp.concatenate([in_grad, bias_grad[:, None], out_grad[:, None]], axis=1)
    return (result, partial_grad)


def seed_from(final, site_cells, site_values):
    fields_count, width_x, width_y, levels_count = final.shape
    columns = width_x * width_y
    flat = final.reshape(fields_count, columns, levels_count)
    column_pick = (
        (site_cells // levels_count)[:, None] == jnp.arange(columns, dtype=jnp.int32)[None, :]
    ).astype(jnp.float32)
    level_pick = (
        (site_cells % levels_count)[:, None] == jnp.arange(levels_count, dtype=jnp.int32)[None, :]
    ).astype(jnp.float32)
    rows = jnp.einsum("sc,fck->sfk", column_pick, flat, precision=PRECISE)
    at_sites = jnp.sum(rows * level_pick[:, None, :], axis=-1)
    misfit = at_sites - site_values.T
    spread_rows = misfit[:, :, None] * level_pick[:, None, :]
    seed = jnp.einsum("sc,sfk->fck", column_pick, spread_rows, precision=PRECISE)
    return seed.reshape(final.shape)


def add_partial(grad_sum, partial_grad):
    return grad_sum + partial_grad


def butterfly_sum(values, axis):
    count = lax.axis_size(axis)
    if count & (count - 1):
        return lax.psum(values, axis)
    step = 1
    while step < count:
        values = values + lax.ppermute(values, axis, [(i, i ^ step) for i in range(count)])
        step *= 2
    return values


HALO = STEPS + 1
BACK_HALO = 2


def body(state, terrain, site_cells, site_values, w_in, b_in, w_out):
    fields_count, width_x, width_y, levels_count = state.shape
    top_code = (levels_count - terrain).astype(jnp.float32)
    code_plane = jnp.broadcast_to(top_code[None, :, :, None], (1, width_x, width_y, levels_count))
    packed = padded_2(jnp.concatenate([state, code_plane], axis=0), (("gx", 1), ("gy", 2)), HALO)
    fields = packed[:fields_count]
    terrain_padded = levels_count - packed[fields_count, :, :, 0].astype(jnp.int32)
    fluid_padded = fluid_cells(terrain_padded, levels_count)
    grad_sum = jnp.zeros((w_in.shape[0], w_in.shape[1] + 2), jnp.float32)
    saved = []
    for step_index in range(STEPS):
        trim = step_index
        terrain_here = crop(terrain_padded, trim, 0)
        fluid_here = crop(fluid_padded, trim, 0)
        viscous = viscosity(hidden_units(closure_inputs(fields, terrain_here), w_in, b_in), w_out)
        saved.append((fields, viscous, fluid_here, terrain_here))
        fields = advance(fields, viscous, fluid_here)
    fields = crop(fields, HALO - STEPS, 1)
    backward = seed_from(fields, site_cells, site_values)
    reach = 0
    for step_index in range(STEPS - 1, -1, -1):
        if reach == 0:
            reach = min(BACK_HALO, step_index + 1)
            backward = padded_2(backward, (("gx", 1), ("gy", 2)), reach)
        padded, viscous, fluid_here, terrain_here = saved[step_index]
        trim = HALO - step_index - reach
        backward, partial_grad = adjoint_step(
            crop(padded, trim, 1),
            crop(viscous, trim, 0),
            crop(fluid_here, trim, 0),
            crop(terrain_here, trim, 0),
            backward,
            w_in,
            b_in,
            w_out,
            reach - 1,
        )
        reach -= 1
        grad_sum = add_partial(grad_sum, partial_grad)
    closure_sum = butterfly_sum(butterfly_sum(grad_sum, "gy"), "gx")
    site_total = site_cells.shape[0] * lax.axis_size("gx") * lax.axis_size("gy")
    return (backward, closure_sum * site_total ** (-0.5))


def solution(mesh):
    return jax.shard_map(
        body,
        mesh=mesh,
        in_specs=(
            P(None, "gx", "gy", None),
            P("gx", "gy"),
            P(("gx", "gy")),
            P(None, ("gx", "gy")),
            P(),
            P(),
            P(),
        ),
        out_specs=(P(None, "gx", "gy", None), P()),
        check_vma=False,
    )
```

```python
import jax
import jax.numpy as jnp
from jax import lax
from jax.sharding import PartitionSpec as P

STEPS = 4


PRECISE = lax.Precision.HIGHEST


def padded_2(cells, sides, width):
    for axis, dim in sides:
        count = lax.axis_size(axis)
        ends = count - 1
        head = lax.slice_in_dim(cells, 0, width, axis=dim)
        tail = lax.slice_in_dim(cells, cells.shape[dim] - width, cells.shape[dim], axis=dim)
        cells = jnp.concatenate(
            [
                lax.ppermute(tail, axis, [(i, (i + 1) % count) for i in range(ends)]),
                cells,
                lax.ppermute(head, axis, [((i + 1) % count, i) for i in range(ends)]),
            ],
            axis=dim,
        )
    return cells


def faces_padded(cells, width):
    parts = []
    for axis, dim in (("gx", 1), ("gy", 2)):
        count = lax.axis_size(axis)
        ends = count - 1
        head = lax.slice_in_dim(cells, 0, width, axis=dim)
        tail = lax.slice_in_dim(cells, cells.shape[dim] - width, cells.shape[dim], axis=dim)
        parts.append(lax.ppermute(tail, axis, [(i, (i + 1) % count) for i in range(ends)]))
        parts.append(lax.ppermute(head, axis, [((i + 1) % count, i) for i in range(ends)]))
    low_x, high_x, low_y, high_y = parts
    middle = jnp.concatenate([low_y, cells, high_y], axis=2)
    shape = list(low_x.shape)
    shape[2] = width
    blank = jnp.zeros(shape, cells.dtype)
    low_x = jnp.concatenate([blank, low_x, blank], axis=2)
    high_x = jnp.concatenate([blank, high_x, blank], axis=2)
    return jnp.concatenate([low_x, middle, high_x], axis=1)


def vertical_diff(values):
    blank = jnp.zeros_like(values[..., :1])
    upper = jnp.concatenate([values[..., 1:], blank], axis=-1)
    lower = jnp.concatenate([blank, values[..., :-1]], axis=-1)
    return 0.5 * (upper - lower)


def closure_inputs(fields, terrain):
    levels = jnp.arange(fields.shape[-1], dtype=jnp.int32)
    height = 2.0 * (levels - terrain[..., None]).astype(jnp.float32) / fields.shape[-1]
    return jnp.stack(
        [vertical_diff(fields[0]), vertical_diff(fields[1]), vertical_diff(fields[2]), height]
    )


def spread(weights, ndim):
    return weights.reshape(weights.shape + (1,) * ndim)


def hidden_units(inputs, w_in, b_in):
    ndim = inputs.ndim - 1
    before = spread(w_in[:, 0], ndim) * inputs[0]
    for feature in range(1, inputs.shape[0]):
        before = before + spread(w_in[:, feature], ndim) * inputs[feature]
    return jnp.tanh(before + spread(b_in, ndim))


def logit_of(hidden, w_out):
    return jnp.sum(spread(w_out, hidden.ndim - 1) * hidden, axis=0)


def viscosity(hidden, w_out):
    return 0.16 * jax.nn.sigmoid(logit_of(hidden, w_out))


def interior(values):
    return values[..., 1:-1, 1:-1, :]


def beside(values):
    return [
        values[..., 2:, 1:-1, :],
        values[..., :-2, 1:-1, :],
        values[..., 1:-1, 2:, :],
        values[..., 1:-1, :-2, :],
    ]


def above_below(values):
    blank = jnp.zeros_like(values[..., :1])
    return [
        jnp.concatenate([values[..., 1:], blank], axis=-1),
        jnp.concatenate([blank, values[..., :-1]], axis=-1),
    ]


def fluid_cells(terrain, levels_count):
    levels = jnp.arange(levels_count, dtype=jnp.int32)
    return (levels >= terrain[..., None]).astype(jnp.float32)


def advance(fields, viscous, fluid):
    centre = interior(fields)
    visc_mid = interior(viscous)
    fluid_mid = interior(fluid)
    near_sets = list(zip(beside(fields), beside(viscous), beside(fluid)))
    near_sets = near_sets + list(
        zip(above_below(centre), above_below(visc_mid), above_below(fluid_mid))
    )
    summed = centre
    for field_near, visc_near, fluid_near in near_sets:
        conductance = fluid_mid * fluid_near * 0.5 * (visc_mid + visc_near)
        summed = summed + conductance * (field_near - centre)
    return summed


def crop(values, count, first):
    if count == 0:
        return values
    for dim in (first, first + 1):
        values = lax.slice_in_dim(values, count, values.shape[dim] - count, axis=dim)
    return values


def adjoint_step(padded, viscous, fluid, terrain, backward, w_in, b_in, w_out, core):
    centre = interior(padded)
    visc_mid = interior(viscous)
    fluid_mid = interior(fluid)
    back_mid = interior(backward)
    near_sets = list(zip(beside(padded), beside(viscous), beside(fluid), beside(backward)))
    near_sets = near_sets + list(
        zip(
            above_below(centre),
            above_below(visc_mid),
            above_below(fluid_mid),
            above_below(back_mid),
        )
    )
    result = back_mid
    visc_grad = jnp.zeros(visc_mid.shape, jnp.float32)
    for field_near, visc_near, fluid_near, back_near in near_sets:
        open_face = fluid_mid * fluid_near
        conductance = open_face * 0.5 * (visc_mid + visc_near)
        result = result + conductance * (back_near - back_mid)
        visc_grad = visc_grad + open_face * 0.5 * jnp.sum(
            (field_near - centre) * (back_mid - back_near), axis=0
        )
    inputs = closure_inputs(centre, terrain[1:-1, 1:-1])
    hidden = hidden_units(inputs, w_in, b_in)
    squash = jax.nn.sigmoid(logit_of(hidden, w_out))
    logit_grad = visc_grad * 0.16 * squash * (1.0 - squash)
    before_grad = spread(w_out, 3) * logit_grad * (1.0 - hidden * hidden)
    logit_core = crop(logit_grad, core, 0)
    hidden_core = crop(hidden, core, 1)
    before_core = crop(before_grad, core, 1)
    inputs_core = crop(inputs, core, 1)
    cells = (1, 2, 3)
    out_grad = jnp.sum(logit_core * hidden_core, axis=cells)
    in_grad = jnp.stack(
        [jnp.sum(before_core * inputs_core[feature], axis=cells) for feature in range(inputs.shape[0])],
        axis=1,
    )
    bias_grad = jnp.sum(before_core, axis=cells)
    input_grad = jnp.stack(
        [jnp.sum(spread(w_in[:, feature], 3) * before_grad, axis=0) for feature in range(3)]
    )
    result = result.at[:3].add(-vertical_diff(input_grad))
    partial_grad = jnp.concatenate([in_grad, bias_grad[:, None], out_grad[:, None]], axis=1)
    return (result, partial_grad)


def seed_from(final, site_cells, site_values):
    fields_count, width_x, width_y, levels_count = final.shape
    columns = width_x * width_y
    flat = final.reshape(fields_count, columns, levels_count)
    column_pick = (
        (site_cells // levels_count)[:, None] == jnp.arange(columns, dtype=jnp.int32)[None, :]
    ).astype(jnp.float32)
    level_pick = (
        (site_cells % levels_count)[:, None] == jnp.arange(levels_count, dtype=jnp.int32)[None, :]
    ).astype(jnp.float32)
    rows = jnp.einsum("sc,fck->sfk", column_pick, flat, precision=PRECISE)
    at_sites = jnp.sum(rows * level_pick[:, None, :], axis=-1)
    misfit = at_sites - site_values.T
    spread_rows = misfit[:, :, None] * level_pick[:, None, :]
    seed = jnp.einsum("sc,sfk->fck", column_pick, spread_rows, precision=PRECISE)
    return seed.reshape(final.shape)


def add_partial(grad_sum, partial_grad):
    return grad_sum + partial_grad


def butterfly_sum(values, axis):
    count = lax.axis_size(axis)
    if count & (count - 1):
        return lax.psum(values, axis)
    step = 1
    while step < count:
        values = values + lax.ppermute(values, axis, [(i, i ^ step) for i in range(count)])
        step *= 2
    return values


HALO = STEPS
BACK_HALO = 2


def body(state, terrain, site_cells, site_values, w_in, b_in, w_out):
    fields_count, width_x, width_y, levels_count = state.shape
    top_code = (levels_count - terrain).astype(jnp.float32)
    code_plane = jnp.broadcast_to(top_code[None, :, :, None], (1, width_x, width_y, levels_count))
    packed = padded_2(jnp.concatenate([state, code_plane], axis=0), (("gx", 1), ("gy", 2)), HALO)
    fields = packed[:fields_count]
    terrain_padded = levels_count - packed[fields_count, :, :, 0].astype(jnp.int32)
    fluid_padded = fluid_cells(terrain_padded, levels_count)
    grad_sum = jnp.zeros((w_in.shape[0], w_in.shape[1] + 2), jnp.float32)
    saved = []
    for step_index in range(STEPS):
        trim = step_index
        terrain_here = crop(terrain_padded, trim, 0)
        fluid_here = crop(fluid_padded, trim, 0)
        viscous = viscosity(hidden_units(closure_inputs(fields, terrain_here), w_in, b_in), w_out)
        saved.append((fields, viscous, fluid_here, terrain_here))
        fields = advance(fields, viscous, fluid_here)
    fields = crop(fields, HALO - STEPS, 1)
    backward = seed_from(fields, site_cells, site_values)
    reach = 0
    for step_index in range(STEPS - 1, -1, -1):
        if reach == 0:
            reach = min(BACK_HALO, step_index + 1, HALO - step_index)
            if reach == 1:
                backward = faces_padded(backward, reach)
            else:
                backward = padded_2(backward, (("gx", 1), ("gy", 2)), reach)
        padded, viscous, fluid_here, terrain_here = saved[step_index]
        trim = HALO - step_index - reach
        backward, partial_grad = adjoint_step(
            crop(padded, trim, 1),
            crop(viscous, trim, 0),
            crop(fluid_here, trim, 0),
            crop(terrain_here, trim, 0),
            backward,
            w_in,
            b_in,
            w_out,
            reach - 1,
        )
        reach -= 1
        grad_sum = add_partial(grad_sum, partial_grad)
    closure_sum = butterfly_sum(butterfly_sum(grad_sum, "gy"), "gx")
    site_total = site_cells.shape[0] * lax.axis_size("gx") * lax.axis_size("gy")
    return (backward, closure_sum * site_total ** (-0.5))


def solution(mesh):
    return jax.shard_map(
        body,
        mesh=mesh,
        in_specs=(
            P(None, "gx", "gy", None),
            P("gx", "gy"),
            P(("gx", "gy")),
            P(None, ("gx", "gy")),
            P(),
            P(),
            P(),
        ),
        out_specs=(P(None, "gx", "gy", None), P()),
        check_vma=False,
    )
```

```python
import jax
import jax.numpy as jnp
from jax import lax
from jax.sharding import PartitionSpec as P

STEPS = 4


PRECISE = lax.Precision.HIGHEST


def padded_2(cells, sides, width):
    for axis, dim in sides:
        count = lax.axis_size(axis)
        ends = count - 1
        head = lax.slice_in_dim(cells, 0, width, axis=dim)
        tail = lax.slice_in_dim(cells, cells.shape[dim] - width, cells.shape[dim], axis=dim)
        cells = jnp.concatenate(
            [
                lax.ppermute(tail, axis, [(i, (i + 1) % count) for i in range(ends)]),
                cells,
                lax.ppermute(head, axis, [((i + 1) % count, i) for i in range(ends)]),
            ],
            axis=dim,
        )
    return cells


def faces_padded(cells, width):
    parts = []
    for axis, dim in (("gx", 1), ("gy", 2)):
        count = lax.axis_size(axis)
        ends = count - 1
        head = lax.slice_in_dim(cells, 0, width, axis=dim)
        tail = lax.slice_in_dim(cells, cells.shape[dim] - width, cells.shape[dim], axis=dim)
        parts.append(lax.ppermute(tail, axis, [(i, (i + 1) % count) for i in range(ends)]))
        parts.append(lax.ppermute(head, axis, [((i + 1) % count, i) for i in range(ends)]))
    low_x, high_x, low_y, high_y = parts
    middle = jnp.concatenate([low_y, cells, high_y], axis=2)
    shape = list(low_x.shape)
    shape[2] = width
    blank = jnp.zeros(shape, cells.dtype)
    low_x = jnp.concatenate([blank, low_x, blank], axis=2)
    high_x = jnp.concatenate([blank, high_x, blank], axis=2)
    return jnp.concatenate([low_x, middle, high_x], axis=1)


def vertical_diff(values):
    blank = jnp.zeros_like(values[..., :1])
    upper = jnp.concatenate([values[..., 1:], blank], axis=-1)
    lower = jnp.concatenate([blank, values[..., :-1]], axis=-1)
    return 0.5 * (upper - lower)


def closure_inputs(fields, terrain):
    levels = jnp.arange(fields.shape[-1], dtype=jnp.int32)
    height = 2.0 * (levels - terrain[..., None]).astype(jnp.float32) / fields.shape[-1]
    return jnp.stack(
        [vertical_diff(fields[0]), vertical_diff(fields[1]), vertical_diff(fields[2]), height]
    )


def spread(weights, ndim):
    return weights.reshape(weights.shape + (1,) * ndim)


def hidden_units(inputs, w_in, b_in):
    ndim = inputs.ndim - 1
    before = spread(w_in[:, 0], ndim) * inputs[0]
    for feature in range(1, inputs.shape[0]):
        before = before + spread(w_in[:, feature], ndim) * inputs[feature]
    return jnp.tanh(before + spread(b_in, ndim))


def logit_of(hidden, w_out):
    return jnp.sum(spread(w_out, hidden.ndim - 1) * hidden, axis=0)


def viscosity(hidden, w_out):
    return 0.16 * jax.nn.sigmoid(logit_of(hidden, w_out))


def interior(values):
    return values[..., 1:-1, 1:-1, :]


def beside(values):
    return [
        values[..., 2:, 1:-1, :],
        values[..., :-2, 1:-1, :],
        values[..., 1:-1, 2:, :],
        values[..., 1:-1, :-2, :],
    ]


def above_below(values):
    blank = jnp.zeros_like(values[..., :1])
    return [
        jnp.concatenate([values[..., 1:], blank], axis=-1),
        jnp.concatenate([blank, values[..., :-1]], axis=-1),
    ]


def fluid_cells(terrain, levels_count):
    levels = jnp.arange(levels_count, dtype=jnp.int32)
    return (levels >= terrain[..., None]).astype(jnp.float32)


def advance(fields, viscous, fluid):
    centre = interior(fields)
    visc_mid = interior(viscous)
    fluid_mid = interior(fluid)
    near_sets = list(zip(beside(fields), beside(viscous), beside(fluid)))
    near_sets = near_sets + list(
        zip(above_below(centre), above_below(visc_mid), above_below(fluid_mid))
    )
    summed = centre
    for field_near, visc_near, fluid_near in near_sets:
        conductance = fluid_mid * fluid_near * 0.5 * (visc_mid + visc_near)
        summed = summed + conductance * (field_near - centre)
    return summed


def crop(values, count, first):
    if count == 0:
        return values
    for dim in (first, first + 1):
        values = lax.slice_in_dim(values, count, values.shape[dim] - count, axis=dim)
    return values


def adjoint_step(padded, viscous, fluid, terrain, backward, w_in, b_in, w_out, core):
    centre = interior(padded)
    visc_mid = interior(viscous)
    fluid_mid = interior(fluid)
    back_mid = interior(backward)
    near_sets = list(zip(beside(padded), beside(viscous), beside(fluid), beside(backward)))
    near_sets = near_sets + list(
        zip(
            above_below(centre),
            above_below(visc_mid),
            above_below(fluid_mid),
            above_below(back_mid),
        )
    )
    result = back_mid
    visc_grad = jnp.zeros(visc_mid.shape, jnp.float32)
    for field_near, visc_near, fluid_near, back_near in near_sets:
        open_face = fluid_mid * fluid_near
        conductance = open_face * 0.5 * (visc_mid + visc_near)
        result = result + conductance * (back_near - back_mid)
        visc_grad = visc_grad + open_face * 0.5 * jnp.sum(
            (field_near - centre) * (back_mid - back_near), axis=0
        )
    inputs = closure_inputs(centre, terrain[1:-1, 1:-1])
    hidden = hidden_units(inputs, w_in, b_in)
    squash = jax.nn.sigmoid(logit_of(hidden, w_out))
    logit_grad = visc_grad * 0.16 * squash * (1.0 - squash)
    before_grad = spread(w_out, 3) * logit_grad * (1.0 - hidden * hidden)
    logit_core = crop(logit_grad, core, 0)
    hidden_core = crop(hidden, core, 1)
    before_core = crop(before_grad, core, 1)
    inputs_core = crop(inputs, core, 1)
    cells = (1, 2, 3)
    out_grad = jnp.sum(logit_core * hidden_core, axis=cells)
    in_grad = jnp.stack(
        [jnp.sum(before_core * inputs_core[feature], axis=cells) for feature in range(inputs.shape[0])],
        axis=1,
    )
    bias_grad = jnp.sum(before_core, axis=cells)
    input_grad = jnp.stack(
        [jnp.sum(spread(w_in[:, feature], 3) * before_grad, axis=0) for feature in range(3)]
    )
    result = result.at[:3].add(-vertical_diff(input_grad))
    partial_grad = jnp.concatenate([in_grad, bias_grad[:, None], out_grad[:, None]], axis=1)
    return (result, partial_grad)


def site_table(site_cells, site_values):
    return jnp.concatenate([site_cells.astype(jnp.float32)[None], site_values], axis=0)


def neighbour_tables(table):
    tables = [(table, 0, 0)]
    for axis, shift_x, shift_y in (("gx", 1, 0), ("gy", 0, 1)):
        count = lax.axis_size(axis)
        ends = count - 1
        low = lax.ppermute(table, axis, [(i, (i + 1) % count) for i in range(ends)])
        high = lax.ppermute(table, axis, [((i + 1) % count, i) for i in range(ends)])
        tables.append((low, -shift_x, -shift_y))
        tables.append((high, shift_x, shift_y))
    return tables


def seed_from(final, tables, width):
    fields_count, region_x, region_y, levels_count = final.shape
    block_x = region_x - 2 * width
    block_y = region_y - 2 * width
    columns = region_x * region_y
    flat = final.reshape(fields_count, columns, levels_count)
    column_ids = []
    level_ids = []
    values = []
    for table, shift_x, shift_y in tables:
        cells = table[0].astype(jnp.int32)
        level = cells % levels_count
        local = cells // levels_count
        at_x = local // block_y + shift_x * block_x + width
        at_y = local % block_y + shift_y * block_y + width
        inside = (at_x >= 0) & (at_x < region_x) & (at_y >= 0) & (at_y < region_y)
        column_ids.append(jnp.where(inside, at_x * region_y + at_y, -1))
        level_ids.append(level)
        values.append(table[1:])
    column_ids = jnp.concatenate(column_ids)
    level_ids = jnp.concatenate(level_ids)
    values = jnp.concatenate(values, axis=1)
    column_pick = (column_ids[:, None] == jnp.arange(columns, dtype=jnp.int32)[None, :]).astype(
        jnp.float32
    )
    level_pick = (
        level_ids[:, None] == jnp.arange(levels_count, dtype=jnp.int32)[None, :]
    ).astype(jnp.float32)
    rows = jnp.einsum("sc,fck->sfk", column_pick, flat, precision=PRECISE)
    at_sites = jnp.sum(rows * level_pick[:, None, :], axis=-1)
    misfit = at_sites - values.T
    spread_rows = misfit[:, :, None] * level_pick[:, None, :]
    seed = jnp.einsum("sc,sfk->fck", column_pick, spread_rows, precision=PRECISE)
    return seed.reshape(final.shape)


def add_partial(grad_sum, partial_grad):
    return grad_sum + partial_grad


def butterfly_sum(values, axis):
    count = lax.axis_size(axis)
    if count & (count - 1):
        return lax.psum(values, axis)
    step = 1
    while step < count:
        values = values + lax.ppermute(values, axis, [(i, i ^ step) for i in range(count)])
        step *= 2
    return values


HALO = STEPS + 1
BACK_HALO = 2


def body(state, terrain, site_cells, site_values, w_in, b_in, w_out):
    fields_count, width_x, width_y, levels_count = state.shape
    top_code = (levels_count - terrain).astype(jnp.float32)
    code_plane = jnp.broadcast_to(top_code[None, :, :, None], (1, width_x, width_y, levels_count))
    packed = padded_2(jnp.concatenate([state, code_plane], axis=0), (("gx", 1), ("gy", 2)), HALO)
    fields = packed[:fields_count]
    tables = neighbour_tables(site_table(site_cells, site_values))
    if HALO == STEPS:
        tables = tables[:1]
    terrain_padded = levels_count - packed[fields_count, :, :, 0].astype(jnp.int32)
    fluid_padded = fluid_cells(terrain_padded, levels_count)
    grad_sum = jnp.zeros((w_in.shape[0], w_in.shape[1] + 2), jnp.float32)
    saved = []
    for step_index in range(STEPS):
        trim = step_index
        terrain_here = crop(terrain_padded, trim, 0)
        fluid_here = crop(fluid_padded, trim, 0)
        viscous = viscosity(hidden_units(closure_inputs(fields, terrain_here), w_in, b_in), w_out)
        saved.append((fields, viscous, fluid_here, terrain_here))
        fields = advance(fields, viscous, fluid_here)
    reach = HALO - STEPS
    backward = seed_from(fields, tables, reach)
    for step_index in range(STEPS - 1, -1, -1):
        if reach == 0:
            reach = min(BACK_HALO, step_index + 1, HALO - step_index)
            if reach == 1:
                backward = faces_padded(backward, reach)
            else:
                backward = padded_2(backward, (("gx", 1), ("gy", 2)), reach)
        padded, viscous, fluid_here, terrain_here = saved[step_index]
        trim = HALO - step_index - reach
        backward, partial_grad = adjoint_step(
            crop(padded, trim, 1),
            crop(viscous, trim, 0),
            crop(fluid_here, trim, 0),
            crop(terrain_here, trim, 0),
            backward,
            w_in,
            b_in,
            w_out,
            reach - 1,
        )
        reach -= 1
        grad_sum = add_partial(grad_sum, partial_grad)
    closure_sum = butterfly_sum(butterfly_sum(grad_sum, "gy"), "gx")
    site_total = site_cells.shape[0] * lax.axis_size("gx") * lax.axis_size("gy")
    return (backward, closure_sum * site_total ** (-0.5))


def solution(mesh):
    return jax.shard_map(
        body,
        mesh=mesh,
        in_specs=(
            P(None, "gx", "gy", None),
            P("gx", "gy"),
            P(("gx", "gy")),
            P(None, ("gx", "gy")),
            P(),
            P(),
            P(),
        ),
        out_specs=(P(None, "gx", "gy", None), P()),
        check_vma=False,
    )
```

```python
import jax
import jax.numpy as jnp
from jax import lax
from jax.sharding import PartitionSpec as P

STEPS = 4


PRECISE = lax.Precision.HIGHEST


def padded_2(cells, sides, width):
    for axis, dim in sides:
        count = lax.axis_size(axis)
        ends = count - 1
        head = lax.slice_in_dim(cells, 0, width, axis=dim)
        tail = lax.slice_in_dim(cells, cells.shape[dim] - width, cells.shape[dim], axis=dim)
        cells = jnp.concatenate(
            [
                lax.ppermute(tail, axis, [(i, (i + 1) % count) for i in range(ends)]),
                cells,
                lax.ppermute(head, axis, [((i + 1) % count, i) for i in range(ends)]),
            ],
            axis=dim,
        )
    return cells


def faces_padded(cells, width):
    parts = []
    for axis, dim in (("gx", 1), ("gy", 2)):
        count = lax.axis_size(axis)
        ends = count - 1
        head = lax.slice_in_dim(cells, 0, width, axis=dim)
        tail = lax.slice_in_dim(cells, cells.shape[dim] - width, cells.shape[dim], axis=dim)
        parts.append(lax.ppermute(tail, axis, [(i, (i + 1) % count) for i in range(ends)]))
        parts.append(lax.ppermute(head, axis, [((i + 1) % count, i) for i in range(ends)]))
    low_x, high_x, low_y, high_y = parts
    middle = jnp.concatenate([low_y, cells, high_y], axis=2)
    shape = list(low_x.shape)
    shape[2] = width
    blank = jnp.zeros(shape, cells.dtype)
    low_x = jnp.concatenate([blank, low_x, blank], axis=2)
    high_x = jnp.concatenate([blank, high_x, blank], axis=2)
    return jnp.concatenate([low_x, middle, high_x], axis=1)


def vertical_diff(values):
    blank = jnp.zeros_like(values[..., :1])
    upper = jnp.concatenate([values[..., 1:], blank], axis=-1)
    lower = jnp.concatenate([blank, values[..., :-1]], axis=-1)
    return 0.5 * (upper - lower)


def closure_inputs(fields, terrain):
    levels = jnp.arange(fields.shape[-1], dtype=jnp.int32)
    height = 2.0 * (levels - terrain[..., None]).astype(jnp.float32) / fields.shape[-1]
    return jnp.stack(
        [vertical_diff(fields[0]), vertical_diff(fields[1]), vertical_diff(fields[2]), height]
    )


def spread(weights, ndim):
    return weights.reshape(weights.shape + (1,) * ndim)


def hidden_units(inputs, w_in, b_in):
    ndim = inputs.ndim - 1
    before = spread(w_in[:, 0], ndim) * inputs[0]
    for feature in range(1, inputs.shape[0]):
        before = before + spread(w_in[:, feature], ndim) * inputs[feature]
    return jnp.tanh(before + spread(b_in, ndim))


def logit_of(hidden, w_out):
    return jnp.sum(spread(w_out, hidden.ndim - 1) * hidden, axis=0)


def viscosity(hidden, w_out):
    return 0.16 * jax.nn.sigmoid(logit_of(hidden, w_out))


def interior(values):
    return values[..., 1:-1, 1:-1, :]


def beside(values):
    return [
        values[..., 2:, 1:-1, :],
        values[..., :-2, 1:-1, :],
        values[..., 1:-1, 2:, :],
        values[..., 1:-1, :-2, :],
    ]


def above_below(values):
    blank = jnp.zeros_like(values[..., :1])
    return [
        jnp.concatenate([values[..., 1:], blank], axis=-1),
        jnp.concatenate([blank, values[..., :-1]], axis=-1),
    ]


def fluid_cells(terrain, levels_count):
    levels = jnp.arange(levels_count, dtype=jnp.int32)
    return (levels >= terrain[..., None]).astype(jnp.float32)


def advance(fields, viscous, fluid):
    centre = interior(fields)
    visc_mid = interior(viscous)
    fluid_mid = interior(fluid)
    near_sets = list(zip(beside(fields), beside(viscous), beside(fluid)))
    near_sets = near_sets + list(
        zip(above_below(centre), above_below(visc_mid), above_below(fluid_mid))
    )
    summed = centre
    for field_near, visc_near, fluid_near in near_sets:
        conductance = fluid_mid * fluid_near * 0.5 * (visc_mid + visc_near)
        summed = summed + conductance * (field_near - centre)
    return summed


def crop(values, count, first):
    if count == 0:
        return values
    for dim in (first, first + 1):
        values = lax.slice_in_dim(values, count, values.shape[dim] - count, axis=dim)
    return values


def adjoint_step(padded, viscous, fluid, terrain, backward, w_in, b_in, w_out, core):
    centre = interior(padded)
    visc_mid = interior(viscous)
    fluid_mid = interior(fluid)
    back_mid = interior(backward)
    near_sets = list(zip(beside(padded), beside(viscous), beside(fluid), beside(backward)))
    near_sets = near_sets + list(
        zip(
            above_below(centre),
            above_below(visc_mid),
            above_below(fluid_mid),
            above_below(back_mid),
        )
    )
    result = back_mid
    visc_grad = jnp.zeros(visc_mid.shape, jnp.float32)
    for field_near, visc_near, fluid_near, back_near in near_sets:
        open_face = fluid_mid * fluid_near
        conductance = open_face * 0.5 * (visc_mid + visc_near)
        result = result + conductance * (back_near - back_mid)
        visc_grad = visc_grad + open_face * 0.5 * jnp.sum(
            (field_near - centre) * (back_mid - back_near), axis=0
        )
    inputs = closure_inputs(centre, terrain[1:-1, 1:-1])
    hidden = hidden_units(inputs, w_in, b_in)
    squash = jax.nn.sigmoid(logit_of(hidden, w_out))
    logit_grad = visc_grad * 0.16 * squash * (1.0 - squash)
    before_grad = spread(w_out, 3) * logit_grad * (1.0 - hidden * hidden)
    logit_core = crop(logit_grad, core, 0)
    hidden_core = crop(hidden, core, 1)
    before_core = crop(before_grad, core, 1)
    inputs_core = crop(inputs, core, 1)
    cells = (1, 2, 3)
    out_grad = jnp.sum(logit_core * hidden_core, axis=cells)
    in_grad = jnp.stack(
        [jnp.sum(before_core * inputs_core[feature], axis=cells) for feature in range(inputs.shape[0])],
        axis=1,
    )
    bias_grad = jnp.sum(before_core, axis=cells)
    input_grad = jnp.stack(
        [jnp.sum(spread(w_in[:, feature], 3) * before_grad, axis=0) for feature in range(3)]
    )
    result = result.at[:3].add(-vertical_diff(input_grad))
    partial_grad = jnp.concatenate([in_grad, bias_grad[:, None], out_grad[:, None]], axis=1)
    return (result, partial_grad)


def site_table(site_cells, site_values):
    return jnp.concatenate([site_cells.astype(jnp.float32)[None], site_values], axis=0)


def neighbour_tables(table):
    tables = [(table, 0, 0)]
    for axis, shift_x, shift_y in (("gx", 1, 0), ("gy", 0, 1)):
        count = lax.axis_size(axis)
        ends = count - 1
        low = lax.ppermute(table, axis, [(i, (i + 1) % count) for i in range(ends)])
        high = lax.ppermute(table, axis, [((i + 1) % count, i) for i in range(ends)])
        tables.append((low, -shift_x, -shift_y))
        tables.append((high, shift_x, shift_y))
    return tables


def seed_from(final, tables, width):
    fields_count, region_x, region_y, levels_count = final.shape
    block_x = region_x - 2 * width
    block_y = region_y - 2 * width
    columns = region_x * region_y
    flat = final.reshape(fields_count, columns, levels_count)
    column_ids = []
    level_ids = []
    values = []
    for table, shift_x, shift_y in tables:
        cells = table[0].astype(jnp.int32)
        level = cells % levels_count
        local = cells // levels_count
        at_x = local // block_y + shift_x * block_x + width
        at_y = local % block_y + shift_y * block_y + width
        inside = (at_x >= 0) & (at_x < region_x) & (at_y >= 0) & (at_y < region_y)
        column_ids.append(jnp.where(inside, at_x * region_y + at_y, -1))
        level_ids.append(level)
        values.append(table[1:])
    column_ids = jnp.concatenate(column_ids)
    level_ids = jnp.concatenate(level_ids)
    values = jnp.concatenate(values, axis=1)
    column_pick = (column_ids[:, None] == jnp.arange(columns, dtype=jnp.int32)[None, :]).astype(
        jnp.float32
    )
    level_pick = (
        level_ids[:, None] == jnp.arange(levels_count, dtype=jnp.int32)[None, :]
    ).astype(jnp.float32)
    rows = jnp.einsum("sc,fck->sfk", column_pick, flat, precision=PRECISE)
    at_sites = jnp.sum(rows * level_pick[:, None, :], axis=-1)
    misfit = at_sites - values.T
    spread_rows = misfit[:, :, None] * level_pick[:, None, :]
    seed = jnp.einsum("sc,sfk->fck", column_pick, spread_rows, precision=PRECISE)
    return seed.reshape(final.shape)


def add_partial(grad_sum, partial_grad):
    return grad_sum + partial_grad


def butterfly_sum(values, axis):
    count = lax.axis_size(axis)
    if count & (count - 1):
        return lax.psum(values, axis)
    step = 1
    while step < count:
        values = values + lax.ppermute(values, axis, [(i, i ^ step) for i in range(count)])
        step *= 2
    return values


HALO = STEPS + 1
BACK_HALO = 2


def body(state, terrain, site_cells, site_values, w_in, b_in, w_out):
    fields_count, width_x, width_y, levels_count = state.shape
    top_code = (levels_count - terrain).astype(jnp.float32)
    code_plane = jnp.broadcast_to(top_code[None, :, :, None], (1, width_x, width_y, levels_count))
    packed = padded_2(jnp.concatenate([state, code_plane], axis=0), (("gx", 1), ("gy", 2)), HALO)
    fields = packed[:fields_count]
    table, packed = lax.optimization_barrier((site_table(site_cells, site_values), packed))
    tables = neighbour_tables(table)
    if HALO == STEPS:
        tables = tables[:1]
    terrain_padded = levels_count - packed[fields_count, :, :, 0].astype(jnp.int32)
    fluid_padded = fluid_cells(terrain_padded, levels_count)
    grad_sum = jnp.zeros((w_in.shape[0], w_in.shape[1] + 2), jnp.float32)
    saved = []
    for step_index in range(STEPS):
        trim = step_index
        terrain_here = crop(terrain_padded, trim, 0)
        fluid_here = crop(fluid_padded, trim, 0)
        viscous = viscosity(hidden_units(closure_inputs(fields, terrain_here), w_in, b_in), w_out)
        saved.append((fields, viscous, fluid_here, terrain_here))
        fields = advance(fields, viscous, fluid_here)
    reach = HALO - STEPS
    backward = seed_from(fields, tables, reach)
    for step_index in range(STEPS - 1, -1, -1):
        if reach == 0:
            reach = min(BACK_HALO, step_index + 1, HALO - step_index)
            if reach == 1:
                backward = faces_padded(backward, reach)
            else:
                backward = padded_2(backward, (("gx", 1), ("gy", 2)), reach)
        padded, viscous, fluid_here, terrain_here = saved[step_index]
        trim = HALO - step_index - reach
        backward, partial_grad = adjoint_step(
            crop(padded, trim, 1),
            crop(viscous, trim, 0),
            crop(fluid_here, trim, 0),
            crop(terrain_here, trim, 0),
            backward,
            w_in,
            b_in,
            w_out,
            reach - 1,
        )
        reach -= 1
        grad_sum = add_partial(grad_sum, partial_grad)
    closure_sum = butterfly_sum(butterfly_sum(grad_sum, "gy"), "gx")
    site_total = site_cells.shape[0] * lax.axis_size("gx") * lax.axis_size("gy")
    return (backward, closure_sum * site_total ** (-0.5))


def solution(mesh):
    return jax.shard_map(
        body,
        mesh=mesh,
        in_specs=(
            P(None, "gx", "gy", None),
            P("gx", "gy"),
            P(("gx", "gy")),
            P(None, ("gx", "gy")),
            P(),
            P(),
            P(),
        ),
        out_specs=(P(None, "gx", "gy", None), P()),
        check_vma=False,
    )
```

```python
import jax
import jax.numpy as jnp
from jax import lax
from jax.sharding import PartitionSpec as P

STEPS = 4


PRECISE = lax.Precision.HIGHEST


def padded_2(cells, sides, width):
    for axis, dim in sides:
        count = lax.axis_size(axis)
        ends = count - 1
        head = lax.slice_in_dim(cells, 0, width, axis=dim)
        tail = lax.slice_in_dim(cells, cells.shape[dim] - width, cells.shape[dim], axis=dim)
        cells = jnp.concatenate(
            [
                lax.ppermute(tail, axis, [(i, (i + 1) % count) for i in range(ends)]),
                cells,
                lax.ppermute(head, axis, [((i + 1) % count, i) for i in range(ends)]),
            ],
            axis=dim,
        )
    return cells


def faces_padded(cells, width):
    parts = []
    for axis, dim in (("gx", 1), ("gy", 2)):
        count = lax.axis_size(axis)
        ends = count - 1
        head = lax.slice_in_dim(cells, 0, width, axis=dim)
        tail = lax.slice_in_dim(cells, cells.shape[dim] - width, cells.shape[dim], axis=dim)
        parts.append(lax.ppermute(tail, axis, [(i, (i + 1) % count) for i in range(ends)]))
        parts.append(lax.ppermute(head, axis, [((i + 1) % count, i) for i in range(ends)]))
    low_x, high_x, low_y, high_y = parts
    middle = jnp.concatenate([low_y, cells, high_y], axis=2)
    shape = list(low_x.shape)
    shape[2] = width
    blank = jnp.zeros(shape, cells.dtype)
    low_x = jnp.concatenate([blank, low_x, blank], axis=2)
    high_x = jnp.concatenate([blank, high_x, blank], axis=2)
    return jnp.concatenate([low_x, middle, high_x], axis=1)


def vertical_diff(values):
    blank = jnp.zeros_like(values[..., :1])
    upper = jnp.concatenate([values[..., 1:], blank], axis=-1)
    lower = jnp.concatenate([blank, values[..., :-1]], axis=-1)
    return 0.5 * (upper - lower)


def closure_inputs(fields, terrain):
    levels = jnp.arange(fields.shape[-1], dtype=jnp.int32)
    height = 2.0 * (levels - terrain[..., None]).astype(jnp.float32) / fields.shape[-1]
    return jnp.stack(
        [vertical_diff(fields[0]), vertical_diff(fields[1]), vertical_diff(fields[2]), height]
    )


def spread(weights, ndim):
    return weights.reshape(weights.shape + (1,) * ndim)


def hidden_units(inputs, w_in, b_in):
    ndim = inputs.ndim - 1
    before = spread(w_in[:, 0], ndim) * inputs[0]
    for feature in range(1, inputs.shape[0]):
        before = before + spread(w_in[:, feature], ndim) * inputs[feature]
    return jnp.tanh(before + spread(b_in, ndim))


def logit_of(hidden, w_out):
    return jnp.sum(spread(w_out, hidden.ndim - 1) * hidden, axis=0)


def viscosity(hidden, w_out):
    return 0.16 * jax.nn.sigmoid(logit_of(hidden, w_out))


def interior(values):
    return values[..., 1:-1, 1:-1, :]


def beside(values):
    return [
        values[..., 2:, 1:-1, :],
        values[..., :-2, 1:-1, :],
        values[..., 1:-1, 2:, :],
        values[..., 1:-1, :-2, :],
    ]


def above_below(values):
    blank = jnp.zeros_like(values[..., :1])
    return [
        jnp.concatenate([values[..., 1:], blank], axis=-1),
        jnp.concatenate([blank, values[..., :-1]], axis=-1),
    ]


def fluid_cells(terrain, levels_count):
    levels = jnp.arange(levels_count, dtype=jnp.int32)
    return (levels >= terrain[..., None]).astype(jnp.float32)


def advance(fields, viscous, fluid):
    centre = interior(fields)
    visc_mid = interior(viscous)
    fluid_mid = interior(fluid)
    near_sets = list(zip(beside(fields), beside(viscous), beside(fluid)))
    near_sets = near_sets + list(
        zip(above_below(centre), above_below(visc_mid), above_below(fluid_mid))
    )
    summed = centre
    for field_near, visc_near, fluid_near in near_sets:
        conductance = fluid_mid * fluid_near * 0.5 * (visc_mid + visc_near)
        summed = summed + conductance * (field_near - centre)
    return summed


def crop(values, count, first):
    if count == 0:
        return values
    for dim in (first, first + 1):
        values = lax.slice_in_dim(values, count, values.shape[dim] - count, axis=dim)
    return values


def adjoint_step(padded, viscous, fluid, terrain, backward, w_in, b_in, w_out, core):
    centre = interior(padded)
    visc_mid = interior(viscous)
    fluid_mid = interior(fluid)
    back_mid = interior(backward)
    near_sets = list(zip(beside(padded), beside(viscous), beside(fluid), beside(backward)))
    near_sets = near_sets + list(
        zip(
            above_below(centre),
            above_below(visc_mid),
            above_below(fluid_mid),
            above_below(back_mid),
        )
    )
    result = back_mid
    visc_grad = jnp.zeros(visc_mid.shape, jnp.float32)
    for field_near, visc_near, fluid_near, back_near in near_sets:
        open_face = fluid_mid * fluid_near
        conductance = open_face * 0.5 * (visc_mid + visc_near)
        result = result + conductance * (back_near - back_mid)
        visc_grad = visc_grad + open_face * 0.5 * jnp.sum(
            (field_near - centre) * (back_mid - back_near), axis=0
        )
    inputs = closure_inputs(centre, terrain[1:-1, 1:-1])
    hidden = hidden_units(inputs, w_in, b_in)
    squash = jax.nn.sigmoid(logit_of(hidden, w_out))
    logit_grad = visc_grad * 0.16 * squash * (1.0 - squash)
    before_grad = spread(w_out, 3) * logit_grad * (1.0 - hidden * hidden)
    logit_core = crop(logit_grad, core, 0)
    hidden_core = crop(hidden, core, 1)
    before_core = crop(before_grad, core, 1)
    inputs_core = crop(inputs, core, 1)
    cells = (1, 2, 3)
    out_grad = jnp.sum(logit_core * hidden_core, axis=cells)
    in_grad = jnp.stack(
        [jnp.sum(before_core * inputs_core[feature], axis=cells) for feature in range(inputs.shape[0])],
        axis=1,
    )
    bias_grad = jnp.sum(before_core, axis=cells)
    input_grad = jnp.stack(
        [jnp.sum(spread(w_in[:, feature], 3) * before_grad, axis=0) for feature in range(3)]
    )
    result = result.at[:3].add(-vertical_diff(input_grad))
    partial_grad = jnp.concatenate([in_grad, bias_grad[:, None], out_grad[:, None]], axis=1)
    return (result, partial_grad)


def seed_from(final, site_cells, site_values):
    fields_count, width_x, width_y, levels_count = final.shape
    columns = width_x * width_y
    flat = final.reshape(fields_count, columns, levels_count)
    column_pick = (
        (site_cells // levels_count)[:, None] == jnp.arange(columns, dtype=jnp.int32)[None, :]
    ).astype(jnp.float32)
    level_pick = (
        (site_cells % levels_count)[:, None] == jnp.arange(levels_count, dtype=jnp.int32)[None, :]
    ).astype(jnp.float32)
    rows = jnp.einsum("sc,fck->sfk", column_pick, flat, precision=PRECISE)
    at_sites = jnp.sum(rows * level_pick[:, None, :], axis=-1)
    misfit = at_sites - site_values.T
    spread_rows = misfit[:, :, None] * level_pick[:, None, :]
    seed = jnp.einsum("sc,sfk->fck", column_pick, spread_rows, precision=PRECISE)
    return seed.reshape(final.shape)


def add_partial(grad_sum, partial_grad):
    return grad_sum + partial_grad


def radix_sum(values, axes, group_bits=2):
    count = 1
    for axis in axes:
        count *= lax.axis_size(axis)
    if count & (count - 1):
        return lax.psum(values, axes)
    bits = count.bit_length() - 1
    for low in range(0, bits, group_bits):
        chosen = list(range(low, min(low + group_bits, bits)))
        group = [values]
        for member in range(1, 1 << len(chosen)):
            mask = sum(1 << bit for place, bit in enumerate(chosen) if (member >> place) & 1)
            group.append(lax.ppermute(values, axes, [(i, i ^ mask) for i in range(count)]))
        while len(group) > 1:
            group = [group[2 * j] + group[2 * j + 1] for j in range(len(group) // 2)]
        values = group[0]
    return values


def butterfly_sum(values, axis):
    count = lax.axis_size(axis)
    if count & (count - 1):
        return lax.psum(values, axis)
    step = 1
    while step < count:
        values = values + lax.ppermute(values, axis, [(i, i ^ step) for i in range(count)])
        step *= 2
    return values


HALO = STEPS
BACK_HALO = 2


def body(state, terrain, site_cells, site_values, w_in, b_in, w_out):
    fields_count, width_x, width_y, levels_count = state.shape
    top_code = (levels_count - terrain).astype(jnp.float32)
    code_plane = jnp.broadcast_to(top_code[None, :, :, None], (1, width_x, width_y, levels_count))
    packed = padded_2(jnp.concatenate([state, code_plane], axis=0), (("gx", 1), ("gy", 2)), HALO)
    fields = packed[:fields_count]
    terrain_padded = levels_count - packed[fields_count, :, :, 0].astype(jnp.int32)
    fluid_padded = fluid_cells(terrain_padded, levels_count)
    grad_sum = jnp.zeros((w_in.shape[0], w_in.shape[1] + 2), jnp.float32)
    saved = []
    for step_index in range(STEPS):
        trim = step_index
        terrain_here = crop(terrain_padded, trim, 0)
        fluid_here = crop(fluid_padded, trim, 0)
        viscous = viscosity(hidden_units(closure_inputs(fields, terrain_here), w_in, b_in), w_out)
        saved.append((fields, viscous, fluid_here, terrain_here))
        fields = advance(fields, viscous, fluid_here)
    fields = crop(fields, HALO - STEPS, 1)
    backward = seed_from(fields, site_cells, site_values)
    reach = 0
    for step_index in range(STEPS - 1, -1, -1):
        if reach == 0:
            reach = min(BACK_HALO, step_index + 1, HALO - step_index)
            if reach == 1:
                backward = faces_padded(backward, reach)
            else:
                backward = padded_2(backward, (("gx", 1), ("gy", 2)), reach)
        padded, viscous, fluid_here, terrain_here = saved[step_index]
        trim = HALO - step_index - reach
        backward, partial_grad = adjoint_step(
            crop(padded, trim, 1),
            crop(viscous, trim, 0),
            crop(fluid_here, trim, 0),
            crop(terrain_here, trim, 0),
            backward,
            w_in,
            b_in,
            w_out,
            reach - 1,
        )
        reach -= 1
        grad_sum = add_partial(grad_sum, partial_grad)
    closure_sum = radix_sum(grad_sum, ("gx", "gy"))
    site_total = site_cells.shape[0] * lax.axis_size("gx") * lax.axis_size("gy")
    return (backward, closure_sum * site_total ** (-0.5))


def solution(mesh):
    return jax.shard_map(
        body,
        mesh=mesh,
        in_specs=(
            P(None, "gx", "gy", None),
            P("gx", "gy"),
            P(("gx", "gy")),
            P(None, ("gx", "gy")),
            P(),
            P(),
            P(),
        ),
        out_specs=(P(None, "gx", "gy", None), P()),
        check_vma=False,
    )
```

```python
import jax
import jax.numpy as jnp
from jax import lax
from jax.sharding import PartitionSpec as P

STEPS = 4


PRECISE = lax.Precision.HIGHEST


def padded_2(cells, sides, width):
    for axis, dim in sides:
        count = lax.axis_size(axis)
        ends = count - 1
        head = lax.slice_in_dim(cells, 0, width, axis=dim)
        tail = lax.slice_in_dim(cells, cells.shape[dim] - width, cells.shape[dim], axis=dim)
        cells = jnp.concatenate(
            [
                lax.ppermute(tail, axis, [(i, (i + 1) % count) for i in range(ends)]),
                cells,
                lax.ppermute(head, axis, [((i + 1) % count, i) for i in range(ends)]),
            ],
            axis=dim,
        )
    return cells


def faces_padded(cells, width):
    parts = []
    for axis, dim in (("gx", 1), ("gy", 2)):
        count = lax.axis_size(axis)
        ends = count - 1
        head = lax.slice_in_dim(cells, 0, width, axis=dim)
        tail = lax.slice_in_dim(cells, cells.shape[dim] - width, cells.shape[dim], axis=dim)
        parts.append(lax.ppermute(tail, axis, [(i, (i + 1) % count) for i in range(ends)]))
        parts.append(lax.ppermute(head, axis, [((i + 1) % count, i) for i in range(ends)]))
    low_x, high_x, low_y, high_y = parts
    middle = jnp.concatenate([low_y, cells, high_y], axis=2)
    shape = list(low_x.shape)
    shape[2] = width
    blank = jnp.zeros(shape, cells.dtype)
    low_x = jnp.concatenate([blank, low_x, blank], axis=2)
    high_x = jnp.concatenate([blank, high_x, blank], axis=2)
    return jnp.concatenate([low_x, middle, high_x], axis=1)


def vertical_diff(values):
    blank = jnp.zeros_like(values[..., :1])
    upper = jnp.concatenate([values[..., 1:], blank], axis=-1)
    lower = jnp.concatenate([blank, values[..., :-1]], axis=-1)
    return 0.5 * (upper - lower)


def closure_inputs(fields, terrain):
    levels = jnp.arange(fields.shape[-1], dtype=jnp.int32)
    height = 2.0 * (levels - terrain[..., None]).astype(jnp.float32) / fields.shape[-1]
    return jnp.stack(
        [vertical_diff(fields[0]), vertical_diff(fields[1]), vertical_diff(fields[2]), height]
    )


def spread(weights, ndim):
    return weights.reshape(weights.shape + (1,) * ndim)


def hidden_units(inputs, w_in, b_in):
    ndim = inputs.ndim - 1
    before = spread(w_in[:, 0], ndim) * inputs[0]
    for feature in range(1, inputs.shape[0]):
        before = before + spread(w_in[:, feature], ndim) * inputs[feature]
    return jnp.tanh(before + spread(b_in, ndim))


def logit_of(hidden, w_out):
    return jnp.sum(spread(w_out, hidden.ndim - 1) * hidden, axis=0)


def viscosity(hidden, w_out):
    return 0.16 * jax.nn.sigmoid(logit_of(hidden, w_out))


def interior(values):
    return values[..., 1:-1, 1:-1, :]


def beside(values):
    return [
        values[..., 2:, 1:-1, :],
        values[..., :-2, 1:-1, :],
        values[..., 1:-1, 2:, :],
        values[..., 1:-1, :-2, :],
    ]


def above_below(values):
    blank = jnp.zeros_like(values[..., :1])
    return [
        jnp.concatenate([values[..., 1:], blank], axis=-1),
        jnp.concatenate([blank, values[..., :-1]], axis=-1),
    ]


def fluid_cells(terrain, levels_count):
    levels = jnp.arange(levels_count, dtype=jnp.int32)
    return (levels >= terrain[..., None]).astype(jnp.float32)


def advance(fields, viscous, fluid):
    centre = interior(fields)
    visc_mid = interior(viscous)
    fluid_mid = interior(fluid)
    near_sets = list(zip(beside(fields), beside(viscous), beside(fluid)))
    near_sets = near_sets + list(
        zip(above_below(centre), above_below(visc_mid), above_below(fluid_mid))
    )
    summed = centre
    for field_near, visc_near, fluid_near in near_sets:
        conductance = fluid_mid * fluid_near * 0.5 * (visc_mid + visc_near)
        summed = summed + conductance * (field_near - centre)
    return summed


def crop(values, count, first):
    if count == 0:
        return values
    for dim in (first, first + 1):
        values = lax.slice_in_dim(values, count, values.shape[dim] - count, axis=dim)
    return values


def adjoint_step(padded, viscous, fluid, terrain, backward, w_in, b_in, w_out, core, split):
    centre = interior(padded)
    visc_mid = interior(viscous)
    fluid_mid = interior(fluid)
    back_mid = interior(backward)
    near_sets = list(zip(beside(padded), beside(viscous), beside(fluid), beside(backward)))
    near_sets = near_sets + list(
        zip(
            above_below(centre),
            above_below(visc_mid),
            above_below(fluid_mid),
            above_below(back_mid),
        )
    )
    result = back_mid
    visc_grad = jnp.zeros(visc_mid.shape, jnp.float32)
    for field_near, visc_near, fluid_near, back_near in near_sets:
        open_face = fluid_mid * fluid_near
        conductance = open_face * 0.5 * (visc_mid + visc_near)
        result = result + conductance * (back_near - back_mid)
        visc_grad = visc_grad + open_face * 0.5 * jnp.sum(
            (field_near - centre) * (back_mid - back_near), axis=0
        )
    inputs = closure_inputs(centre, terrain[1:-1, 1:-1])
    hidden = hidden_units(inputs, w_in, b_in)
    squash = jax.nn.sigmoid(logit_of(hidden, w_out))
    logit_grad = visc_grad * 0.16 * squash * (1.0 - squash)
    before_grad = spread(w_out, 3) * logit_grad * (1.0 - hidden * hidden)
    logit_core = crop(logit_grad, core, 0)
    hidden_core = crop(hidden, core, 1)
    before_core = crop(before_grad, core, 1)
    inputs_core = crop(inputs, core, 1)
    cells = (1, 2, 3)
    out_grad = jnp.sum(logit_core * hidden_core, axis=cells)
    in_grad = jnp.stack(
        [jnp.sum(before_core * inputs_core[feature], axis=cells) for feature in range(inputs.shape[0])],
        axis=1,
    )
    bias_grad = jnp.sum(before_core, axis=cells)
    partial_grad = jnp.concatenate([in_grad, bias_grad[:, None], out_grad[:, None]], axis=1)
    if split:
        partial_grad, before_grad = lax.optimization_barrier((partial_grad, before_grad))
    input_grad = jnp.stack(
        [jnp.sum(spread(w_in[:, feature], 3) * before_grad, axis=0) for feature in range(3)]
    )
    result = result.at[:3].add(-vertical_diff(input_grad))
    return (result, partial_grad)


def seed_from(final, site_cells, site_values):
    fields_count, width_x, width_y, levels_count = final.shape
    columns = width_x * width_y
    flat = final.reshape(fields_count, columns, levels_count)
    column_pick = (
        (site_cells // levels_count)[:, None] == jnp.arange(columns, dtype=jnp.int32)[None, :]
    ).astype(jnp.float32)
    level_pick = (
        (site_cells % levels_count)[:, None] == jnp.arange(levels_count, dtype=jnp.int32)[None, :]
    ).astype(jnp.float32)
    rows = jnp.einsum("sc,fck->sfk", column_pick, flat, precision=PRECISE)
    at_sites = jnp.sum(rows * level_pick[:, None, :], axis=-1)
    misfit = at_sites - site_values.T
    spread_rows = misfit[:, :, None] * level_pick[:, None, :]
    seed = jnp.einsum("sc,sfk->fck", column_pick, spread_rows, precision=PRECISE)
    return seed.reshape(final.shape)


def add_partial(grad_sum, partial_grad):
    return grad_sum + partial_grad


def butterfly_sum(values, axis):
    count = lax.axis_size(axis)
    if count & (count - 1):
        return lax.psum(values, axis)
    step = 1
    while step < count:
        values = values + lax.ppermute(values, axis, [(i, i ^ step) for i in range(count)])
        step *= 2
    return values


HALO = STEPS
BACK_HALO = 2


def body(state, terrain, site_cells, site_values, w_in, b_in, w_out):
    fields_count, width_x, width_y, levels_count = state.shape
    top_code = (levels_count - terrain).astype(jnp.float32)
    code_plane = jnp.broadcast_to(top_code[None, :, :, None], (1, width_x, width_y, levels_count))
    packed = padded_2(jnp.concatenate([state, code_plane], axis=0), (("gx", 1), ("gy", 2)), HALO)
    fields = packed[:fields_count]
    terrain_padded = levels_count - packed[fields_count, :, :, 0].astype(jnp.int32)
    fluid_padded = fluid_cells(terrain_padded, levels_count)
    grad_sum = jnp.zeros((w_in.shape[0], w_in.shape[1] + 2), jnp.float32)
    saved = []
    for step_index in range(STEPS):
        trim = step_index
        terrain_here = crop(terrain_padded, trim, 0)
        fluid_here = crop(fluid_padded, trim, 0)
        viscous = viscosity(hidden_units(closure_inputs(fields, terrain_here), w_in, b_in), w_out)
        saved.append((fields, viscous, fluid_here, terrain_here))
        fields = advance(fields, viscous, fluid_here)
    fields = crop(fields, HALO - STEPS, 1)
    backward = seed_from(fields, site_cells, site_values)
    reach = 0
    for step_index in range(STEPS - 1, -1, -1):
        if reach == 0:
            reach = min(BACK_HALO, step_index + 1, HALO - step_index)
            if reach == 1:
                backward = faces_padded(backward, reach)
            else:
                backward = padded_2(backward, (("gx", 1), ("gy", 2)), reach)
        padded, viscous, fluid_here, terrain_here = saved[step_index]
        trim = HALO - step_index - reach
        backward, partial_grad = adjoint_step(
            crop(padded, trim, 1),
            crop(viscous, trim, 0),
            crop(fluid_here, trim, 0),
            crop(terrain_here, trim, 0),
            backward,
            w_in,
            b_in,
            w_out,
            reach - 1,
            step_index == 0,
        )
        reach -= 1
        grad_sum = add_partial(grad_sum, partial_grad)
    closure_sum = butterfly_sum(butterfly_sum(grad_sum, "gy"), "gx")
    site_total = site_cells.shape[0] * lax.axis_size("gx") * lax.axis_size("gy")
    return (backward, closure_sum * site_total ** (-0.5))


def solution(mesh):
    return jax.shard_map(
        body,
        mesh=mesh,
        in_specs=(
            P(None, "gx", "gy", None),
            P("gx", "gy"),
            P(("gx", "gy")),
            P(None, ("gx", "gy")),
            P(),
            P(),
            P(),
        ),
        out_specs=(P(None, "gx", "gy", None), P()),
        check_vma=False,
    )
```

```python
import jax
import jax.numpy as jnp
from jax import lax
from jax.sharding import PartitionSpec as P

STEPS = 4


PRECISE = lax.Precision.HIGHEST


def padded_2(cells, sides, width):
    for axis, dim in sides:
        count = lax.axis_size(axis)
        ends = count - 1
        head = lax.slice_in_dim(cells, 0, width, axis=dim)
        tail = lax.slice_in_dim(cells, cells.shape[dim] - width, cells.shape[dim], axis=dim)
        cells = jnp.concatenate(
            [
                lax.ppermute(tail, axis, [(i, (i + 1) % count) for i in range(ends)]),
                cells,
                lax.ppermute(head, axis, [((i + 1) % count, i) for i in range(ends)]),
            ],
            axis=dim,
        )
    return cells


def faces_padded(cells, width):
    parts = []
    for axis, dim in (("gx", 1), ("gy", 2)):
        count = lax.axis_size(axis)
        ends = count - 1
        head = lax.slice_in_dim(cells, 0, width, axis=dim)
        tail = lax.slice_in_dim(cells, cells.shape[dim] - width, cells.shape[dim], axis=dim)
        parts.append(lax.ppermute(tail, axis, [(i, (i + 1) % count) for i in range(ends)]))
        parts.append(lax.ppermute(head, axis, [((i + 1) % count, i) for i in range(ends)]))
    low_x, high_x, low_y, high_y = parts
    middle = jnp.concatenate([low_y, cells, high_y], axis=2)
    edge = ((0, 0), (0, 0), (width, width), (0, 0))
    return jnp.concatenate([jnp.pad(low_x, edge), middle, jnp.pad(high_x, edge)], axis=1)


def vertical_diff(values):
    blank = jnp.zeros_like(values[..., :1])
    upper = jnp.concatenate([values[..., 1:], blank], axis=-1)
    lower = jnp.concatenate([blank, values[..., :-1]], axis=-1)
    return 0.5 * (upper - lower)


def closure_inputs(fields, terrain):
    levels = jnp.arange(fields.shape[-1], dtype=jnp.int32)
    height = 2.0 * (levels - terrain[..., None]).astype(jnp.float32) / fields.shape[-1]
    return jnp.stack(
        [vertical_diff(fields[0]), vertical_diff(fields[1]), vertical_diff(fields[2]), height]
    )


def spread(weights, ndim):
    return weights.reshape(weights.shape + (1,) * ndim)


def hidden_units(inputs, w_in, b_in):
    ndim = inputs.ndim - 1
    before = spread(w_in[:, 0], ndim) * inputs[0]
    for feature in range(1, inputs.shape[0]):
        before = before + spread(w_in[:, feature], ndim) * inputs[feature]
    return jnp.tanh(before + spread(b_in, ndim))


def logit_of(hidden, w_out):
    return jnp.sum(spread(w_out, hidden.ndim - 1) * hidden, axis=0)


def viscosity(hidden, w_out):
    return 0.16 * jax.nn.sigmoid(logit_of(hidden, w_out))


def interior(values):
    return values[..., 1:-1, 1:-1, :]


def beside(values):
    return [
        values[..., 2:, 1:-1, :],
        values[..., :-2, 1:-1, :],
        values[..., 1:-1, 2:, :],
        values[..., 1:-1, :-2, :],
    ]


def above_below(values):
    blank = jnp.zeros_like(values[..., :1])
    return [
        jnp.concatenate([values[..., 1:], blank], axis=-1),
        jnp.concatenate([blank, values[..., :-1]], axis=-1),
    ]


def fluid_cells(terrain, levels_count):
    levels = jnp.arange(levels_count, dtype=jnp.int32)
    return (levels >= terrain[..., None]).astype(jnp.float32)


def advance(fields, viscous, fluid):
    centre = interior(fields)
    visc_mid = interior(viscous)
    fluid_mid = interior(fluid)
    near_sets = list(zip(beside(fields), beside(viscous), beside(fluid)))
    near_sets = near_sets + list(
        zip(above_below(centre), above_below(visc_mid), above_below(fluid_mid))
    )
    summed = centre
    for field_near, visc_near, fluid_near in near_sets:
        conductance = fluid_mid * fluid_near * 0.5 * (visc_mid + visc_near)
        summed = summed + conductance * (field_near - centre)
    return summed


def crop(values, count, first):
    if count == 0:
        return values
    for dim in (first, first + 1):
        values = lax.slice_in_dim(values, count, values.shape[dim] - count, axis=dim)
    return values


def adjoint_step(padded, viscous, fluid, terrain, backward, w_in, b_in, w_out, core):
    centre = interior(padded)
    visc_mid = interior(viscous)
    fluid_mid = interior(fluid)
    back_mid = interior(backward)
    near_sets = list(zip(beside(padded), beside(viscous), beside(fluid), beside(backward)))
    near_sets = near_sets + list(
        zip(
            above_below(centre),
            above_below(visc_mid),
            above_below(fluid_mid),
            above_below(back_mid),
        )
    )
    result = back_mid
    visc_grad = jnp.zeros(visc_mid.shape, jnp.float32)
    for field_near, visc_near, fluid_near, back_near in near_sets:
        open_face = fluid_mid * fluid_near
        conductance = open_face * 0.5 * (visc_mid + visc_near)
        result = result + conductance * (back_near - back_mid)
        visc_grad = visc_grad + open_face * 0.5 * jnp.sum(
            (field_near - centre) * (back_mid - back_near), axis=0
        )
    inputs = closure_inputs(centre, terrain[1:-1, 1:-1])
    hidden = hidden_units(inputs, w_in, b_in)
    squash = jax.nn.sigmoid(logit_of(hidden, w_out))
    logit_grad = visc_grad * 0.16 * squash * (1.0 - squash)
    before_grad = spread(w_out, 3) * logit_grad * (1.0 - hidden * hidden)
    logit_core = crop(logit_grad, core, 0)
    hidden_core = crop(hidden, core, 1)
    before_core = crop(before_grad, core, 1)
    inputs_core = crop(inputs, core, 1)
    cells = (1, 2, 3)
    out_grad = jnp.sum(logit_core * hidden_core, axis=cells)
    in_grad = jnp.stack(
        [jnp.sum(before_core * inputs_core[feature], axis=cells) for feature in range(inputs.shape[0])],
        axis=1,
    )
    bias_grad = jnp.sum(before_core, axis=cells)
    input_grad = jnp.stack(
        [jnp.sum(spread(w_in[:, feature], 3) * before_grad, axis=0) for feature in range(3)]
    )
    result = result.at[:3].add(-vertical_diff(input_grad))
    partial_grad = jnp.concatenate([in_grad, bias_grad[:, None], out_grad[:, None]], axis=1)
    return (result, partial_grad)


def seed_from(final, site_cells, site_values):
    fields_count, width_x, width_y, levels_count = final.shape
    columns = width_x * width_y
    flat = final.reshape(fields_count, columns, levels_count)
    column_pick = (
        (site_cells // levels_count)[:, None] == jnp.arange(columns, dtype=jnp.int32)[None, :]
    ).astype(jnp.float32)
    level_pick = (
        (site_cells % levels_count)[:, None] == jnp.arange(levels_count, dtype=jnp.int32)[None, :]
    ).astype(jnp.float32)
    rows = jnp.einsum("sc,fck->sfk", column_pick, flat, precision=PRECISE)
    at_sites = jnp.sum(rows * level_pick[:, None, :], axis=-1)
    misfit = at_sites - site_values.T
    spread_rows = misfit[:, :, None] * level_pick[:, None, :]
    seed = jnp.einsum("sc,sfk->fck", column_pick, spread_rows, precision=PRECISE)
    return seed.reshape(final.shape)


def add_partial(grad_sum, partial_grad):
    return grad_sum + partial_grad


def butterfly_sum(values, axis):
    count = lax.axis_size(axis)
    if count & (count - 1):
        return lax.psum(values, axis)
    step = 1
    while step < count:
        values = values + lax.ppermute(values, axis, [(i, i ^ step) for i in range(count)])
        step *= 2
    return values


HALO = STEPS
BACK_HALO = 2


def body(state, terrain, site_cells, site_values, w_in, b_in, w_out):
    fields_count, width_x, width_y, levels_count = state.shape
    top_code = (levels_count - terrain).astype(jnp.float32)
    code_plane = jnp.broadcast_to(top_code[None, :, :, None], (1, width_x, width_y, levels_count))
    packed = padded_2(jnp.concatenate([state, code_plane], axis=0), (("gx", 1), ("gy", 2)), HALO)
    fields = packed[:fields_count]
    terrain_padded = levels_count - packed[fields_count, :, :, 0].astype(jnp.int32)
    fluid_padded = fluid_cells(terrain_padded, levels_count)
    grad_sum = jnp.zeros((w_in.shape[0], w_in.shape[1] + 2), jnp.float32)
    saved = []
    for step_index in range(STEPS):
        trim = step_index
        terrain_here = crop(terrain_padded, trim, 0)
        fluid_here = crop(fluid_padded, trim, 0)
        viscous = viscosity(hidden_units(closure_inputs(fields, terrain_here), w_in, b_in), w_out)
        saved.append((fields, viscous, fluid_here, terrain_here))
        fields = advance(fields, viscous, fluid_here)
    fields = crop(fields, HALO - STEPS, 1)
    backward = seed_from(fields, site_cells, site_values)
    reach = 0
    for step_index in range(STEPS - 1, -1, -1):
        if reach == 0:
            reach = min(BACK_HALO, step_index + 1, HALO - step_index)
            if reach == 1:
                backward = faces_padded(backward, reach)
            else:
                backward = padded_2(backward, (("gx", 1), ("gy", 2)), reach)
        padded, viscous, fluid_here, terrain_here = saved[step_index]
        trim = HALO - step_index - reach
        backward, partial_grad = adjoint_step(
            crop(padded, trim, 1),
            crop(viscous, trim, 0),
            crop(fluid_here, trim, 0),
            crop(terrain_here, trim, 0),
            backward,
            w_in,
            b_in,
            w_out,
            reach - 1,
        )
        reach -= 1
        grad_sum = add_partial(grad_sum, partial_grad)
    closure_sum = butterfly_sum(butterfly_sum(grad_sum, "gy"), "gx")
    site_total = site_cells.shape[0] * lax.axis_size("gx") * lax.axis_size("gy")
    return (backward, closure_sum * site_total ** (-0.5))


def solution(mesh):
    return jax.shard_map(
        body,
        mesh=mesh,
        in_specs=(
            P(None, "gx", "gy", None),
            P("gx", "gy"),
            P(("gx", "gy")),
            P(None, ("gx", "gy")),
            P(),
            P(),
            P(),
        ),
        out_specs=(P(None, "gx", "gy", None), P()),
        check_vma=False,
    )
```
